256 devices in a mesh: lat: 16 (over y_hi, z), lon: 16 (over y_lo, x, core).
Axes of the slice: x: 4, y: 4 (y_hi: 2, y_lo: 2; y = y_hi * 2 + y_lo), z: 8, core: 2. Of those that a mesh axis runs over, the one named last changes fastest.
Arguments:
- grid_tokens: bfloat16 [384, 768, 512], P('lat', 'lon'), may hold values from -28 to 28
- attention_gain: float32 [512], replicated, may hold values from 0.25 to 1.75
- score_weight: bfloat16 [512, 1024], replicated, as said below
- value_weight: bfloat16 [512, 512], replicated, may hold values from -0.25 to 0.25
- output_weight: bfloat16 [512, 512], replicated, may hold values from -0.75 to 0.75
- mixer_gain: float32 [512], replicated, may hold values from 0.25 to 1.75
- first_weight: float32 [2, 8, 64, 64], replicated, may hold values from -0.5 to 0.5
- first_bias: float32 [2, 8, 64], replicated, may hold values from -0.75 to 0.75
- second_weight: float32 [2, 8, 64, 64], replicated, may hold values from -0.5 to 0.5
- second_bias: float32 [2, 8, 64], replicated, may hold values from -0.875 to 0.875
Outputs:
- block_out: bfloat16 [384, 768, 512], P('lat', 'lon')
The draws below stay inside these ranges and needn't reach their ends.
Inputs may be any that keep to these rules, and one draw needn't show every extreme that they name: `score_weight`: every entry lies within 61 / sqrt(512) of zero.
All inputs are finite; a program needn't handle non-finite values.
Results may differ from the reference program's by a relative error of at most 0.0095.
The reference program's roundings to bfloat16 on the way count: a program that leaves them out, or rounds other values in their place, can miss the bound.
Values may be sent and summed in bfloat16 or wider, within the bound.
No kernel may reach another device: no remote copies, remote signals or barrier semaphores. Data moves between devices by JAX's collectives and lax.ppermute only.
A program may use at most 192 MiB of HBM per device.

```python
import math
import jax
import jax.numpy as jnp
from jax import lax

D = 512
HEADS = 8
HD = 64
NB = 8
BS = 64
RADIUS = 6
NH = 384
NW = 768
KQ = 96
KH = 192
MW = 192


def draw_grid_tokens(key, part):
    base_key = jax.random.fold_in(key, 0)
    field = jnp.clip(jax.random.normal(base_key, (NH, NW, D), jnp.float32), -6.0, 6.0)
    return field.astype(jnp.bfloat16)


def draw_score_weight(key, part):
    query_key, key_key = jax.random.split(key, 2)
    factor = 1.0 / math.sqrt(D)
    query_part = jnp.clip(jax.random.normal(query_key, (D, D), jnp.float32), -6.0, 6.0) * factor
    second = jnp.clip(jax.random.normal(key_key, (D, D), jnp.float32), -6.0, 6.0) * factor
    return jnp.concatenate([query_part, second], axis=1).astype(jnp.bfloat16)


def normal_values(stream_key, shape, deviation, limit, kind=jnp.bfloat16):
    entries = jax.random.normal(stream_key, shape, jnp.float32) * deviation
    return jnp.minimum(jnp.maximum(entries, -limit), limit).astype(kind)


def setup_inputs(seed: int = 0) -> dict:
    seeds = jax.random.split(jax.random.key(seed), 11)
    grid_tokens = draw_grid_tokens(jax.random.fold_in(seeds[10], 71), 0)
    attention_gain = jnp.clip(1.0 + 0.15 * jax.random.normal(seeds[1], (D,), jnp.float32), 0.25, 1.75)
    score_weight = draw_score_weight(jax.random.fold_in(seeds[10], 71), 0)
    value_weight = normal_values(seeds[3], (D, D), D ** -0.5, 0.25)
    output_weight = normal_values(seeds[4], (D, D), (D // 8) ** -0.5, 0.75)
    mixer_gain = jnp.clip(1.0 + 0.15 * jax.random.normal(seeds[5], (D,), jnp.float32), 0.25, 1.75)
    first_weight = normal_values(seeds[6], (2, NB, BS, BS), (2 * BS) ** -0.5, 0.5, jnp.float32)
    first_bias = normal_values(seeds[7], (2, NB, BS), 0.05, 0.75, jnp.float32)
    second_weight = normal_values(seeds[8], (2, NB, BS, BS), (2 * BS) ** -0.5, 0.5, jnp.float32)
    second_bias = normal_values(seeds[9], (2, NB, BS), 0.06, 0.875, jnp.float32)
    return dict(grid_tokens=grid_tokens, attention_gain=attention_gain, score_weight=score_weight, value_weight=value_weight, output_weight=output_weight, mixer_gain=mixer_gain, first_weight=first_weight, first_bias=first_bias, second_weight=second_weight, second_bias=second_bias)


HIGHEST = lax.Precision.HIGHEST

def normed(values, gain):
    data = values.astype(jnp.float32)
    centre = lax.optimization_barrier(jnp.mean(data, axis=-1, keepdims=True))
    centred = data - centre
    spread = lax.optimization_barrier(jnp.mean(centred * centred, axis=-1, keepdims=True))
    return (centred * lax.rsqrt(spread + 1e-05) * gain).astype(jnp.bfloat16)

def windowed(stacked):
    queries = stacked[0].astype(jnp.float32)
    keys = stacked[1].astype(jnp.float32)
    values = stacked[2].astype(jnp.float32)
    span = 2 * RADIUS + 1
    first = jnp.clip(jnp.arange(NH, dtype=jnp.int32) - RADIUS, 0, NH - span)
    scores = []
    for down in range(span):
        key_rows = jnp.take(keys, first + down, axis=0)
        for across in range(span):
            shifted = jnp.roll(key_rows, RADIUS - across, axis=1)
            scores.append(lax.optimization_barrier(jnp.sum(queries * shifted, axis=-1)))
    scores = jnp.stack(scores) / math.sqrt(HD)
    largest = lax.optimization_barrier(jnp.max(scores, axis=0))
    weights = jnp.exp(scores - largest)
    rounded = lax.optimization_barrier((weights / lax.optimization_barrier(jnp.sum(weights, axis=0))).astype(jnp.bfloat16))
    probs = rounded.astype(jnp.float32)
    total = jnp.zeros_like(queries)
    for down in range(span):
        value_rows = jnp.take(values, first + down, axis=0)
        for across in range(span):
            shifted = jnp.roll(value_rows, RADIUS - across, axis=1)
            total = total + probs[down * span + across][:, :, None] * shifted
    return total

def split_heads(matrix):
    return jnp.transpose(matrix.reshape(NH, NW, HEADS, HD), (2, 0, 1, 3))

def block_mix(inputs, weight):
    return jnp.einsum('kmbi,bio->kmbo', inputs, weight, precision=HIGHEST)

def reference(grid_tokens, attention_gain, score_weight, value_weight, output_weight, mixer_gain, first_weight, first_bias, second_weight, second_bias):
    normed_in = normed(grid_tokens, attention_gain).reshape(NH * NW, D)
    queries = jnp.dot(normed_in, score_weight[:, :D], preferred_element_type=jnp.float32).astype(jnp.bfloat16)
    keys = jnp.dot(normed_in, score_weight[:, D:], preferred_element_type=jnp.float32).astype(jnp.bfloat16)
    values = jnp.dot(normed_in, value_weight, preferred_element_type=jnp.float32).astype(jnp.bfloat16)
    stacked = jnp.stack([split_heads(queries), split_heads(keys), split_heads(values)], axis=1)
    per_head = lax.map(windowed, stacked)
    attended = jnp.transpose(per_head, (1, 2, 0, 3)).reshape(NH * NW, D).astype(jnp.bfloat16)
    projected = jnp.dot(attended, output_weight, preferred_element_type=jnp.float32)
    after_attention = (grid_tokens.astype(jnp.float32).reshape(NH * NW, D) + projected).astype(jnp.bfloat16).reshape(NH, NW, D)
    mixer_in = normed(after_attention, mixer_gain)
    full = jnp.fft.rfft2(mixer_in.astype(jnp.float32), axes=(0, 1), norm='ortho')
    kept = jnp.concatenate([jnp.arange(KQ, dtype=jnp.int32), jnp.arange(NH - KQ, NH, dtype=jnp.int32)])
    part = full[kept, :MW]
    real_in = jnp.real(part).reshape(KH, MW, NB, BS)
    imag_in = jnp.imag(part).reshape(KH, MW, NB, BS)
    hidden_r = jax.nn.relu(block_mix(real_in, first_weight[0]) - block_mix(imag_in, first_weight[1]) + first_bias[0])
    hidden_i = jax.nn.relu(block_mix(imag_in, first_weight[0]) + block_mix(real_in, first_weight[1]) + first_bias[1])
    filtered_r = block_mix(hidden_r, second_weight[0]) - block_mix(hidden_i, second_weight[1]) + second_bias[0]
    filtered_i = block_mix(hidden_i, second_weight[0]) + block_mix(hidden_r, second_weight[1]) + second_bias[1]
    filtered = (filtered_r + 1j * filtered_i).reshape(KH, MW, D)
    placed = jnp.zeros((NH, NW // 2 + 1, D), filtered.dtype).at[kept, :MW].set(filtered)
    spectral = jnp.fft.irfft2(placed, s=(NH, NW), axes=(0, 1), norm='ortho').astype(jnp.bfloat16)
    summed = after_attention.astype(jnp.float32) + mixer_in.astype(jnp.float32) + spectral.astype(jnp.float32)
    return summed.astype(jnp.bfloat16)
```

```python
import math

import jax
import jax.numpy as jnp
from jax import lax
from jax.sharding import PartitionSpec as P

HEADS = 8
NB = 8
RADIUS = 6


HIGHEST = lax.Precision.HIGHEST
THREE_PASS = lax.Precision.HIGH


def padded_2(cells, sides, width):
    for axis, dim in sides:
        count = lax.axis_size(axis)
        head = lax.slice_in_dim(cells, 0, width, axis=dim)
        tail = lax.slice_in_dim(cells, cells.shape[dim] - width, cells.shape[dim], axis=dim)
        cells = jnp.concatenate(
            [
                lax.ppermute(tail, axis, [(i, (i + 1) % count) for i in range(count)]),
                cells,
                lax.ppermute(head, axis, [((i + 1) % count, i) for i in range(count)]),
            ],
            axis=dim,
        )
    return cells


def normed(values, gain):
    data = values.astype(jnp.float32)
    centre = jnp.mean(data, axis=-1, keepdims=True)
    centred = data - centre
    spread = jnp.mean(centred * centred, axis=-1, keepdims=True)
    return (centred * lax.rsqrt(spread + 1e-05) * gain).astype(jnp.bfloat16)


def mode_tables(total_rows, total_cols, kept_rows, kept_cols):
    factor = 1.0 / math.sqrt(total_rows * total_cols)
    column = jnp.arange(total_cols, dtype=jnp.int32)[:, None]
    lon_freq = jnp.arange(kept_cols, dtype=jnp.int32)[None, :]
    lon_angle = 2.0 * math.pi / total_cols * (column * lon_freq % total_cols).astype(jnp.float32)
    lon_cos = jnp.cos(lon_angle)
    lon_sin = jnp.sin(lon_angle)
    forward_lon = jnp.concatenate([lon_cos, -lon_sin], axis=1) * factor
    doubled = jnp.where(lon_freq == 0, 1.0, 2.0).astype(jnp.float32)
    inverse_lon = (
        jnp.concatenate(
            [jnp.transpose(lon_cos * doubled), jnp.transpose(-lon_sin * doubled)], axis=0
        )
        * factor
    )
    lat_slot = jnp.arange(kept_rows, dtype=jnp.int32)
    lat_freq = lat_slot + jnp.where(lat_slot >= kept_rows // 2, total_rows - kept_rows, 0)
    row_index = jnp.arange(total_rows, dtype=jnp.int32)[:, None]
    lat_angle = (
        2.0
        * math.pi
        / total_rows
        * (row_index * lat_freq[None, :] % total_rows).astype(jnp.float32)
    )
    return (forward_lon, inverse_lon, jnp.cos(lat_angle), jnp.sin(lat_angle))


def block_mix(inputs, weight):
    return jnp.einsum("bim,bio->bom", inputs, weight, precision=HIGHEST)


def shards(
    grid_tokens,
    attention_gain,
    score_weight,
    value_weight,
    output_weight,
    mixer_gain,
    first_weight,
    first_bias,
    second_weight,
    second_bias,
):
    tile_rows, tile_cols, features = grid_tokens.shape
    lat_count = lax.axis_size("lat")
    lon_count = lax.axis_size("lon")
    total_rows = tile_rows * lat_count
    total_cols = tile_cols * lon_count
    head_size = features // HEADS
    span = 2 * RADIUS + 1
    normed_in = normed(grid_tokens, attention_gain)
    flat_in = normed_in.reshape(tile_rows * tile_cols, features)
    queries = jnp.dot(
        flat_in, score_weight[:, :features], preferred_element_type=jnp.float32
    ).astype(jnp.bfloat16)
    queries = queries.reshape(tile_rows, tile_cols, features)
    kv_weight = jnp.concatenate([score_weight[:, features:], value_weight], axis=1)
    projected = jnp.dot(flat_in, kv_weight, preferred_element_type=jnp.float32).astype(jnp.bfloat16)
    projected = projected.reshape(tile_rows, tile_cols, 2 * features)
    padded = padded_2(projected, (("lat", 0), ("lon", 1)), RADIUS)
    key_pad = padded[:, :, :features]
    value_pad = padded[:, :, features:]
    block_rows = 12
    pad_cols = tile_cols + 2 * RADIUS
    row_anchor = lax.axis_index("lat") * tile_rows
    column_gap = (
        jnp.arange(pad_cols, dtype=jnp.int32)[None, :]
        - jnp.arange(tile_cols, dtype=jnp.int32)[:, None]
    )
    column_inside = (column_gap >= 0) & (column_gap < span)
    factor = 1.0 / math.sqrt(head_size)
    pieces = []
    for row_start in range(0, tile_rows, block_rows):
        query_rows = row_anchor + row_start + jnp.arange(block_rows, dtype=jnp.int32)
        window_start = jnp.clip(query_rows - RADIUS, 0, total_rows - span)
        key_rows = (
            row_anchor + row_start - RADIUS + jnp.arange(block_rows + 2 * RADIUS, dtype=jnp.int32)
        )
        row_inside = (key_rows[None, :] >= window_start[:, None]) & (
            key_rows[None, :] < window_start[:, None] + span
        )
        allowed = (row_inside[:, None, :, None] & column_inside[None, :, None, :]).reshape(
            block_rows * tile_cols, -1
        )
        query_block = queries[row_start : row_start + block_rows].reshape(-1, features)
        key_block = key_pad[row_start : row_start + block_rows + 2 * RADIUS].reshape(-1, features)
        value_block = value_pad[row_start : row_start + block_rows + 2 * RADIUS].reshape(
            -1, features
        )
        head_outputs = []
        for head_index in range(HEADS):
            lower = head_index * head_size
            upper = lower + head_size
            scores = (
                jnp.einsum(
                    "qd,kd->qk",
                    query_block[:, lower:upper],
                    key_block[:, lower:upper],
                    preferred_element_type=jnp.float32,
                )
                * factor
            )
            scores = jnp.where(allowed, scores, -1e30)
            largest = jnp.max(scores, axis=1, keepdims=True)
            weights = jnp.exp(scores - largest)
            probs = (weights / jnp.sum(weights, axis=1, keepdims=True)).astype(jnp.bfloat16)
            head_outputs.append(
                jnp.dot(
                    probs, value_block[:, lower:upper], preferred_element_type=jnp.float32
                ).astype(jnp.bfloat16)
            )
        pieces.append(jnp.concatenate(head_outputs, axis=1))
    attended = jnp.concatenate(pieces, axis=0)
    projected_out = jnp.dot(attended, output_weight, preferred_element_type=jnp.float32)
    after_attention = (
        grid_tokens.astype(jnp.float32).reshape(-1, features) + projected_out
    ).astype(jnp.bfloat16)
    after_attention = after_attention.reshape(tile_rows, tile_cols, features)
    mixer_in = normed(after_attention, mixer_gain)
    tile_back = spectral_mix(
        mixer_in, first_weight, first_bias, second_weight, second_bias
    )
    summed = (
        after_attention.astype(jnp.float32)
        + mixer_in.astype(jnp.float32)
        + tile_back.astype(jnp.float32)
    )
    return summed.astype(jnp.bfloat16)


def split_bf16(table):
    high = table.astype(jnp.bfloat16)
    return high, (table - high.astype(jnp.float32)).astype(jnp.bfloat16)


def two_pass(spec, data, table):
    high, rest = split_bf16(table)
    return jnp.einsum(spec, data, high, preferred_element_type=jnp.float32) + jnp.einsum(
        spec, data, rest, preferred_element_type=jnp.float32
    )


def spectral_mix(mixer_in, first_weight, first_bias, second_weight, second_bias):
    tile_rows, tile_cols, features = mixer_in.shape
    lat_count = lax.axis_size("lat")
    lon_count = lax.axis_size("lon")
    total_rows = tile_rows * lat_count
    total_cols = tile_cols * lon_count
    kept_rows = total_rows // 2
    kept_cols = total_cols // 4
    share = features // lon_count
    block = features // NB
    mode_share = kept_cols // lat_count
    forward_lon, inverse_lon, lat_cos, lat_sin = mode_tables(
        total_rows, total_cols, kept_rows, kept_cols
    )
    send = jnp.transpose(
        mixer_in.reshape(tile_rows, tile_cols, lon_count, share), (2, 3, 0, 1)
    )
    got = lax.all_to_all(send, "lon", 0, 0, tiled=True)
    along_lon = two_pass(
        "scrw,swn->rcn", got, forward_lon.reshape(lon_count, tile_cols, 2 * kept_cols)
    )
    along_lon = along_lon.reshape(tile_rows, share, 2, lat_count, mode_share)
    outgoing = jnp.transpose(along_lon, (3, 0, 1, 2, 4)).astype(jnp.bfloat16)
    outgoing = outgoing.reshape(lat_count, tile_rows, share * 2 * mode_share)
    columns = lax.all_to_all(outgoing, "lat", 0, 0, tiled=True)
    columns = columns.reshape(total_rows, share * 2 * mode_share)
    lat_table = jnp.concatenate([lat_cos, lat_sin], axis=1)
    both = two_pass("in,it->tn", columns, lat_table)
    both = both.reshape(2, kept_rows, share, 2, mode_share)
    spec_real = both[0, :, :, 0] + both[1, :, :, 1]
    spec_imag = both[0, :, :, 1] - both[1, :, :, 0]
    spectrum = jnp.stack([spec_real, spec_imag])
    lon_index = lax.axis_index("lon")
    half = lon_index % 2
    block_index = lon_index // 2
    pairs = [(i, i ^ 1) for i in range(lon_count)]
    half_rows = kept_rows // 2
    own = lax.dynamic_slice_in_dim(spectrum, half * half_rows, half_rows, axis=1)
    away = lax.dynamic_slice_in_dim(spectrum, (1 - half) * half_rows, half_rows, axis=1)
    came = lax.ppermute(away, "lon", pairs)
    modes = jnp.where(
        half == 0,
        jnp.concatenate([own, came], axis=2),
        jnp.concatenate([came, own], axis=2),
    )
    w1 = lax.dynamic_index_in_dim(first_weight, block_index, axis=1, keepdims=False)
    b1 = lax.dynamic_index_in_dim(first_bias, block_index, axis=1, keepdims=False)
    w2 = lax.dynamic_index_in_dim(second_weight, block_index, axis=1, keepdims=False)
    b2 = lax.dynamic_index_in_dim(second_bias, block_index, axis=1, keepdims=False)
    real_in, imag_in = modes[0], modes[1]
    hidden_r = jax.nn.relu(
        mode_mix(real_in, w1[0]) - mode_mix(imag_in, w1[1]) + b1[0][None, :, None]
    )
    hidden_i = jax.nn.relu(
        mode_mix(imag_in, w1[0]) + mode_mix(real_in, w1[1]) + b1[1][None, :, None]
    )
    filtered_r = mode_mix(hidden_r, w2[0]) - mode_mix(hidden_i, w2[1]) + b2[0][None, :, None]
    filtered_i = mode_mix(hidden_i, w2[0]) + mode_mix(hidden_r, w2[1]) + b2[1][None, :, None]
    filtered = jnp.stack([filtered_r, filtered_i])
    mine = lax.dynamic_slice_in_dim(filtered, half * share, share, axis=2)
    theirs = lax.dynamic_slice_in_dim(filtered, (1 - half) * share, share, axis=2)
    back = lax.ppermute(theirs, "lon", pairs)
    returned = jnp.where(
        half == 0,
        jnp.concatenate([mine, back], axis=1),
        jnp.concatenate([back, mine], axis=1),
    )
    cos_back = jnp.einsum("ik,pkcm->ipcm", lat_cos, returned, precision=THREE_PASS)
    sin_back = jnp.einsum("ik,pkcm->ipcm", lat_sin, returned, precision=THREE_PASS)
    rows_real = cos_back[:, 0] - sin_back[:, 1]
    rows_imag = sin_back[:, 0] + cos_back[:, 1]
    rows = jnp.stack([rows_real, rows_imag], axis=2).astype(jnp.bfloat16)
    rows = rows.reshape(lat_count, tile_rows, share * 2 * mode_share)
    arrived = lax.all_to_all(rows, "lat", 0, 0, tiled=True)
    arrived = arrived.reshape(lat_count, tile_rows, share, 2, mode_share)
    field = two_pass(
        "srcpm,psmj->rcj",
        arrived,
        inverse_lon.reshape(2, lat_count, mode_share, total_cols),
    ).astype(jnp.bfloat16)
    field = jnp.transpose(
        field.reshape(tile_rows, share, lon_count, tile_cols), (2, 0, 3, 1)
    )
    home = lax.all_to_all(field, "lon", 0, 0, tiled=True)
    return jnp.transpose(home, (1, 2, 0, 3)).reshape(tile_rows, tile_cols, features)


def mode_mix(inputs, weight):
    return jnp.einsum("kcm,co->kom", inputs, weight, precision=HIGHEST)


def solution(mesh):
    placed = (P("lat", "lon", None), P(), P(), P(), P(), P(), P(), P(), P(), P())
    return jax.shard_map(
        shards, mesh=mesh, in_specs=placed, out_specs=P("lat", "lon", None), check_vma=False
    )
```

```python
import math

import jax
import jax.numpy as jnp
from jax import lax
from jax.sharding import PartitionSpec as P

HEADS = 8
NB = 8
RADIUS = 6


HIGHEST = lax.Precision.HIGHEST
THREE_PASS = lax.Precision.HIGH


def padded_2(cells, sides, width):
    for axis, dim in sides:
        count = lax.axis_size(axis)
        head = lax.slice_in_dim(cells, 0, width, axis=dim)
        tail = lax.slice_in_dim(cells, cells.shape[dim] - width, cells.shape[dim], axis=dim)
        cells = jnp.concatenate(
            [
                lax.ppermute(tail, axis, [(i, (i + 1) % count) for i in range(count)]),
                cells,
                lax.ppermute(head, axis, [((i + 1) % count, i) for i in range(count)]),
            ],
            axis=dim,
        )
    return cells


def normed(values, gain):
    data = values.astype(jnp.float32)
    centre = jnp.mean(data, axis=-1, keepdims=True)
    centred = data - centre
    spread = jnp.mean(centred * centred, axis=-1, keepdims=True)
    return (centred * lax.rsqrt(spread + 1e-05) * gain).astype(jnp.bfloat16)


def mode_tables(total_rows, total_cols, kept_rows, kept_cols):
    factor = 1.0 / math.sqrt(total_rows * total_cols)
    column = jnp.arange(total_cols, dtype=jnp.int32)[:, None]
    lon_freq = jnp.arange(kept_cols, dtype=jnp.int32)[None, :]
    lon_angle = 2.0 * math.pi / total_cols * (column * lon_freq % total_cols).astype(jnp.float32)
    lon_cos = jnp.cos(lon_angle)
    lon_sin = jnp.sin(lon_angle)
    forward_lon = jnp.concatenate([lon_cos, -lon_sin], axis=1) * factor
    doubled = jnp.where(lon_freq == 0, 1.0, 2.0).astype(jnp.float32)
    inverse_lon = (
        jnp.concatenate(
            [jnp.transpose(lon_cos * doubled), jnp.transpose(-lon_sin * doubled)], axis=0
        )
        * factor
    )
    lat_slot = jnp.arange(kept_rows, dtype=jnp.int32)
    lat_freq = lat_slot + jnp.where(lat_slot >= kept_rows // 2, total_rows - kept_rows, 0)
    row_index = jnp.arange(total_rows, dtype=jnp.int32)[:, None]
    lat_angle = (
        2.0
        * math.pi
        / total_rows
        * (row_index * lat_freq[None, :] % total_rows).astype(jnp.float32)
    )
    return (forward_lon, inverse_lon, jnp.cos(lat_angle), jnp.sin(lat_angle))


def block_mix(inputs, weight):
    return jnp.einsum("bim,bio->bom", inputs, weight, precision=HIGHEST)


def shards(
    grid_tokens,
    attention_gain,
    score_weight,
    value_weight,
    output_weight,
    mixer_gain,
    first_weight,
    first_bias,
    second_weight,
    second_bias,
):
    tile_rows, tile_cols, features = grid_tokens.shape
    lat_count = lax.axis_size("lat")
    lon_count = lax.axis_size("lon")
    total_rows = tile_rows * lat_count
    total_cols = tile_cols * lon_count
    head_size = features // HEADS
    span = 2 * RADIUS + 1
    normed_in = normed(grid_tokens, attention_gain)
    flat_in = normed_in.reshape(tile_rows * tile_cols, features)
    queries = jnp.dot(
        flat_in, score_weight[:, :features], preferred_element_type=jnp.float32
    ).astype(jnp.bfloat16)
    queries = queries.reshape(tile_rows, tile_cols, features)
    kv_weight = jnp.concatenate([score_weight[:, features:], value_weight], axis=1)
    projected = jnp.dot(flat_in, kv_weight, preferred_element_type=jnp.float32).astype(jnp.bfloat16)
    projected = projected.reshape(tile_rows, tile_cols, 2 * features)
    padded = padded_2(projected, (("lat", 0), ("lon", 1)), RADIUS)
    key_pad = padded[:, :, :features]
    value_pad = padded[:, :, features:]
    block_rows = 12
    block_cols = tile_cols // 2
    row_anchor = lax.axis_index("lat") * tile_rows
    column_gap = (
        jnp.arange(block_cols + 2 * RADIUS, dtype=jnp.int32)[None, :]
        - jnp.arange(block_cols, dtype=jnp.int32)[:, None]
    )
    column_inside = (column_gap >= 0) & (column_gap < span)
    factor = 1.0 / math.sqrt(head_size)
    pieces = []
    for row_start in range(0, tile_rows, block_rows):
        query_rows = row_anchor + row_start + jnp.arange(block_rows, dtype=jnp.int32)
        window_start = jnp.clip(query_rows - RADIUS, 0, total_rows - span)
        key_rows = (
            row_anchor + row_start - RADIUS + jnp.arange(block_rows + 2 * RADIUS, dtype=jnp.int32)
        )
        row_inside = (key_rows[None, :] >= window_start[:, None]) & (
            key_rows[None, :] < window_start[:, None] + span
        )
        allowed = (row_inside[:, None, :, None] & column_inside[None, :, None, :]).reshape(
            block_rows * block_cols, -1
        )
        row_pieces = []
        for col_start in range(0, tile_cols, block_cols):
            query_block = queries[
                row_start : row_start + block_rows, col_start : col_start + block_cols
            ].reshape(-1, features)
            key_block = key_pad[
                row_start : row_start + block_rows + 2 * RADIUS,
                col_start : col_start + block_cols + 2 * RADIUS,
            ].reshape(-1, features)
            value_block = value_pad[
                row_start : row_start + block_rows + 2 * RADIUS,
                col_start : col_start + block_cols + 2 * RADIUS,
            ].reshape(-1, features)
            head_outputs = []
            for head_index in range(HEADS):
                lower = head_index * head_size
                upper = lower + head_size
                scores = (
                    jnp.einsum(
                        "qd,kd->qk",
                        query_block[:, lower:upper],
                        key_block[:, lower:upper],
                        preferred_element_type=jnp.float32,
                    )
                    * factor
                )
                scores = jnp.where(allowed, scores, -1e30)
                largest = jnp.max(scores, axis=1, keepdims=True)
                weights = jnp.exp(scores - largest)
                probs = (weights / jnp.sum(weights, axis=1, keepdims=True)).astype(jnp.bfloat16)
                head_outputs.append(
                    jnp.dot(
                        probs, value_block[:, lower:upper], preferred_element_type=jnp.float32
                    ).astype(jnp.bfloat16)
                )
            row_pieces.append(
                jnp.concatenate(head_outputs, axis=1).reshape(block_rows, block_cols, features)
            )
        pieces.append(jnp.concatenate(row_pieces, axis=1).reshape(-1, features))
    attended = jnp.concatenate(pieces, axis=0)
    projected_out = jnp.dot(attended, output_weight, preferred_element_type=jnp.float32)
    after_attention = (
        grid_tokens.astype(jnp.float32).reshape(-1, features) + projected_out
    ).astype(jnp.bfloat16)
    after_attention = after_attention.reshape(tile_rows, tile_cols, features)
    mixer_in = lax.optimization_barrier(normed(after_attention, mixer_gain))
    tile_back = spectral_mix(
        mixer_in, first_weight, first_bias, second_weight, second_bias
    )
    summed = (
        after_attention.astype(jnp.float32)
        + mixer_in.astype(jnp.float32)
        + tile_back.astype(jnp.float32)
    )
    return summed.astype(jnp.bfloat16)


def split_bf16(table):
    high = table.astype(jnp.bfloat16)
    return high, (table - high.astype(jnp.float32)).astype(jnp.bfloat16)


def two_pass(spec, data, table):
    high, rest = split_bf16(table)
    return jnp.einsum(spec, data, high, preferred_element_type=jnp.float32) + jnp.einsum(
        spec, data, rest, preferred_element_type=jnp.float32
    )


def spectral_mix(mixer_in, first_weight, first_bias, second_weight, second_bias):
    tile_rows, tile_cols, features = mixer_in.shape
    lat_count = lax.axis_size("lat")
    lon_count = lax.axis_size("lon")
    total_rows = tile_rows * lat_count
    total_cols = tile_cols * lon_count
    kept_rows = total_rows // 2
    kept_cols = total_cols // 4
    share = features // lon_count
    block = features // NB
    mode_share = kept_cols // lat_count
    forward_lon, inverse_lon, lat_cos, lat_sin = mode_tables(
        total_rows, total_cols, kept_rows, kept_cols
    )
    send = jnp.transpose(
        mixer_in.reshape(tile_rows, tile_cols, lon_count, share), (2, 3, 0, 1)
    )
    got = lax.all_to_all(send, "lon", 0, 0, tiled=True)
    along_lon = two_pass(
        "scrw,swn->rcn", got, forward_lon.reshape(lon_count, tile_cols, 2 * kept_cols)
    )
    along_lon = along_lon.reshape(tile_rows, share, 2, lat_count, mode_share)
    outgoing = jnp.transpose(along_lon, (3, 0, 1, 2, 4)).astype(jnp.bfloat16)
    outgoing = outgoing.reshape(lat_count, tile_rows, share * 2 * mode_share)
    columns = lax.all_to_all(outgoing, "lat", 0, 0, tiled=True)
    columns = columns.reshape(total_rows, share * 2 * mode_share)
    lat_table = jnp.concatenate([lat_cos, lat_sin], axis=1)
    both = two_pass("in,it->tn", columns, lat_table)
    both = both.reshape(2, kept_rows, share, 2, mode_share)
    spec_real = both[0, :, :, 0] + both[1, :, :, 1]
    spec_imag = both[0, :, :, 1] - both[1, :, :, 0]
    spectrum = jnp.stack([spec_real, spec_imag])
    lon_index = lax.axis_index("lon")
    half = lon_index % 2
    block_index = lon_index // 2
    pairs = [(i, i ^ 1) for i in range(lon_count)]
    half_rows = kept_rows // 2
    own = lax.dynamic_slice_in_dim(spectrum, half * half_rows, half_rows, axis=1)
    away = lax.dynamic_slice_in_dim(spectrum, (1 - half) * half_rows, half_rows, axis=1)
    came = lax.ppermute(away, "lon", pairs)
    modes = jnp.where(
        half == 0,
        jnp.concatenate([own, came], axis=2),
        jnp.concatenate([came, own], axis=2),
    )
    w1 = lax.dynamic_index_in_dim(first_weight, block_index, axis=1, keepdims=False)
    b1 = lax.dynamic_index_in_dim(first_bias, block_index, axis=1, keepdims=False)
    w2 = lax.dynamic_index_in_dim(second_weight, block_index, axis=1, keepdims=False)
    b2 = lax.dynamic_index_in_dim(second_bias, block_index, axis=1, keepdims=False)
    real_in, imag_in = modes[0], modes[1]
    hidden_r = jax.nn.relu(
        mode_mix(real_in, w1[0]) - mode_mix(imag_in, w1[1]) + b1[0][None, :, None]
    )
    hidden_i = jax.nn.relu(
        mode_mix(imag_in, w1[0]) + mode_mix(real_in, w1[1]) + b1[1][None, :, None]
    )
    filtered_r = mode_mix(hidden_r, w2[0]) - mode_mix(hidden_i, w2[1]) + b2[0][None, :, None]
    filtered_i = mode_mix(hidden_i, w2[0]) + mode_mix(hidden_r, w2[1]) + b2[1][None, :, None]
    filtered = jnp.stack([filtered_r, filtered_i])
    mine = lax.dynamic_slice_in_dim(filtered, half * share, share, axis=2)
    theirs = lax.dynamic_slice_in_dim(filtered, (1 - half) * share, share, axis=2)
    back = lax.ppermute(theirs, "lon", pairs)
    returned = jnp.where(
        half == 0,
        jnp.concatenate([mine, back], axis=1),
        jnp.concatenate([back, mine], axis=1),
    )
    cos_back = jnp.einsum("ik,pkcm->ipcm", lat_cos, returned, precision=THREE_PASS)
    sin_back = jnp.einsum("ik,pkcm->ipcm", lat_sin, returned, precision=THREE_PASS)
    rows_real = cos_back[:, 0] - sin_back[:, 1]
    rows_imag = sin_back[:, 0] + cos_back[:, 1]
    rows = jnp.stack([rows_real, rows_imag], axis=2).astype(jnp.bfloat16)
    rows = rows.reshape(lat_count, tile_rows, share * 2 * mode_share)
    arrived = lax.all_to_all(rows, "lat", 0, 0, tiled=True)
    arrived = arrived.reshape(lat_count, tile_rows, share, 2, mode_share)
    field = two_pass(
        "srcpm,psmj->rcj",
        arrived,
        inverse_lon.reshape(2, lat_count, mode_share, total_cols),
    ).astype(jnp.bfloat16)
    field = jnp.transpose(
        field.reshape(tile_rows, share, lon_count, tile_cols), (2, 0, 3, 1)
    )
    home = lax.all_to_all(field, "lon", 0, 0, tiled=True)
    return lax.optimization_barrier(
        jnp.transpose(home, (1, 2, 0, 3)).reshape(tile_rows, tile_cols, features)
    )


def mode_mix(inputs, weight):
    return jnp.einsum("kcm,co->kom", inputs, weight, precision=HIGHEST)


def solution(mesh):
    placed = (P("lat", "lon", None), P(), P(), P(), P(), P(), P(), P(), P(), P())
    return jax.shard_map(
        shards, mesh=mesh, in_specs=placed, out_specs=P("lat", "lon", None), check_vma=False
    )
```

```python
import math

import jax
import jax.numpy as jnp
from jax import lax
from jax.sharding import PartitionSpec as P

HEADS = 8
NB = 8
RADIUS = 6


HIGHEST = lax.Precision.HIGHEST
THREE_PASS = lax.Precision.HIGH


def padded_2(cells, sides, width):
    for axis, dim in sides:
        count = lax.axis_size(axis)
        head = lax.slice_in_dim(cells, 0, width, axis=dim)
        tail = lax.slice_in_dim(cells, cells.shape[dim] - width, cells.shape[dim], axis=dim)
        cells = jnp.concatenate(
            [
                lax.ppermute(tail, axis, [(i, (i + 1) % count) for i in range(count)]),
                cells,
                lax.ppermute(head, axis, [((i + 1) % count, i) for i in range(count)]),
            ],
            axis=dim,
        )
    return cells


def normed(values, gain):
    data = values.astype(jnp.float32)
    centre = jnp.mean(data, axis=-1, keepdims=True)
    centred = data - centre
    spread = jnp.mean(centred * centred, axis=-1, keepdims=True)
    return (centred * lax.rsqrt(spread + 1e-05) * gain).astype(jnp.bfloat16)


def mode_tables(total_rows, total_cols, kept_rows, kept_cols):
    factor = 1.0 / math.sqrt(total_rows * total_cols)
    column = jnp.arange(total_cols, dtype=jnp.int32)[:, None]
    lon_freq = jnp.arange(kept_cols, dtype=jnp.int32)[None, :]
    lon_angle = 2.0 * math.pi / total_cols * (column * lon_freq % total_cols).astype(jnp.float32)
    lon_cos = jnp.cos(lon_angle)
    lon_sin = jnp.sin(lon_angle)
    forward_lon = jnp.concatenate([lon_cos, -lon_sin], axis=1) * factor
    doubled = jnp.where(lon_freq == 0, 1.0, 2.0).astype(jnp.float32)
    inverse_lon = (
        jnp.concatenate(
            [jnp.transpose(lon_cos * doubled), jnp.transpose(-lon_sin * doubled)], axis=0
        )
        * factor
    )
    lat_slot = jnp.arange(kept_rows, dtype=jnp.int32)
    lat_freq = lat_slot + jnp.where(lat_slot >= kept_rows // 2, total_rows - kept_rows, 0)
    row_index = jnp.arange(total_rows, dtype=jnp.int32)[:, None]
    lat_angle = (
        2.0
        * math.pi
        / total_rows
        * (row_index * lat_freq[None, :] % total_rows).astype(jnp.float32)
    )
    return (forward_lon, inverse_lon, jnp.cos(lat_angle), jnp.sin(lat_angle))


def block_mix(inputs, weight):
    return jnp.einsum("bim,bio->bom", inputs, weight, precision=HIGHEST)


def shards(
    grid_tokens,
    attention_gain,
    score_weight,
    value_weight,
    output_weight,
    mixer_gain,
    first_weight,
    first_bias,
    second_weight,
    second_bias,
):
    tile_rows, tile_cols, features = grid_tokens.shape
    lat_count = lax.axis_size("lat")
    lon_count = lax.axis_size("lon")
    total_rows = tile_rows * lat_count
    total_cols = tile_cols * lon_count
    head_size = features // HEADS
    span = 2 * RADIUS + 1
    normed_in = normed(grid_tokens, attention_gain)
    flat_in = normed_in.reshape(tile_rows * tile_cols, features)
    queries = jnp.dot(
        flat_in, score_weight[:, :features], preferred_element_type=jnp.float32
    ).astype(jnp.bfloat16)
    queries = queries.reshape(tile_rows, tile_cols, features)
    kv_weight = jnp.concatenate([score_weight[:, features:], value_weight], axis=1)
    projected = jnp.dot(flat_in, kv_weight, preferred_element_type=jnp.float32).astype(jnp.bfloat16)
    projected = projected.reshape(tile_rows, tile_cols, 2 * features)
    padded = padded_2(projected, (("lat", 0), ("lon", 1)), RADIUS)
    key_pad = padded[:, :, :features]
    value_pad = padded[:, :, features:]
    block_rows = 12
    block_cols = tile_cols // 2
    row_blocks = tile_rows // block_rows
    col_blocks = tile_cols // block_cols
    key_rows_block = block_rows + 2 * RADIUS
    key_cols_block = block_cols + 2 * RADIUS
    row_anchor = lax.axis_index("lat") * tile_rows
    column_gap = (
        jnp.arange(key_cols_block, dtype=jnp.int32)[None, :]
        - jnp.arange(block_cols, dtype=jnp.int32)[:, None]
    )
    column_inside = (column_gap >= 0) & (column_gap < span)
    query_rows = row_anchor + jnp.arange(tile_rows, dtype=jnp.int32).reshape(row_blocks, block_rows)
    window_start = jnp.clip(query_rows - RADIUS, 0, total_rows - span)
    key_rows = (
        row_anchor
        - RADIUS
        + block_rows * jnp.arange(row_blocks, dtype=jnp.int32)[:, None]
        + jnp.arange(key_rows_block, dtype=jnp.int32)[None, :]
    )
    row_inside = (key_rows[:, None, :] >= window_start[:, :, None]) & (
        key_rows[:, None, :] < window_start[:, :, None] + span
    )
    allowed = (
        row_inside[:, None, :, None, :, None] & column_inside[None, None, None, :, None, :]
    )
    allowed = jnp.broadcast_to(
        allowed,
        (row_blocks, col_blocks, block_rows, block_cols, key_rows_block, key_cols_block),
    ).reshape(row_blocks * col_blocks, block_rows * block_cols, key_rows_block * key_cols_block)
    factor = 1.0 / math.sqrt(head_size)
    query_blocks = jnp.transpose(
        queries.reshape(row_blocks, block_rows, col_blocks, block_cols, features), (0, 2, 1, 3, 4)
    ).reshape(row_blocks * col_blocks, block_rows * block_cols, features)

    def gathered(table):
        return jnp.stack(
            [
                table[
                    r * block_rows : r * block_rows + key_rows_block,
                    c * block_cols : c * block_cols + key_cols_block,
                ].reshape(-1, features)
                for r in range(row_blocks)
                for c in range(col_blocks)
            ]
        )

    key_blocks = gathered(key_pad)
    value_blocks = gathered(value_pad)
    head_outputs = []
    for head_index in range(HEADS):
        lower = head_index * head_size
        upper = lower + head_size
        scores = (
            jnp.einsum(
                "bqd,bkd->bqk",
                query_blocks[:, :, lower:upper],
                key_blocks[:, :, lower:upper],
                preferred_element_type=jnp.float32,
            )
            * factor
        )
        scores = jnp.where(allowed, scores, -1e30)
        largest = jnp.max(scores, axis=2, keepdims=True)
        weights = jnp.exp(scores - largest)
        probs = (weights / jnp.sum(weights, axis=2, keepdims=True)).astype(jnp.bfloat16)
        head_outputs.append(
            jnp.einsum(
                "bqk,bkd->bqd",
                probs,
                value_blocks[:, :, lower:upper],
                preferred_element_type=jnp.float32,
            ).astype(jnp.bfloat16)
        )
    attended = jnp.concatenate(head_outputs, axis=2).reshape(
        row_blocks, col_blocks, block_rows, block_cols, features
    )
    attended = jnp.transpose(attended, (0, 2, 1, 3, 4)).reshape(-1, features)
    projected_out = jnp.dot(attended, output_weight, preferred_element_type=jnp.float32)
    after_attention = (
        grid_tokens.astype(jnp.float32).reshape(-1, features) + projected_out
    ).astype(jnp.bfloat16)
    after_attention = after_attention.reshape(tile_rows, tile_cols, features)
    mixer_in = lax.optimization_barrier(normed(after_attention, mixer_gain))
    tile_back = spectral_mix(
        mixer_in, first_weight, first_bias, second_weight, second_bias
    )
    summed = (
        after_attention.astype(jnp.float32)
        + mixer_in.astype(jnp.float32)
        + tile_back.astype(jnp.float32)
    )
    return summed.astype(jnp.bfloat16)


def split_bf16(table):
    high = table.astype(jnp.bfloat16)
    return high, (table - high.astype(jnp.float32)).astype(jnp.bfloat16)


def two_pass(spec, data, table):
    high, rest = split_bf16(table)
    return jnp.einsum(spec, data, high, preferred_element_type=jnp.float32) + jnp.einsum(
        spec, data, rest, preferred_element_type=jnp.float32
    )


def spectral_mix(mixer_in, first_weight, first_bias, second_weight, second_bias):
    tile_rows, tile_cols, features = mixer_in.shape
    lat_count = lax.axis_size("lat")
    lon_count = lax.axis_size("lon")
    total_rows = tile_rows * lat_count
    total_cols = tile_cols * lon_count
    kept_rows = total_rows // 2
    kept_cols = total_cols // 4
    share = features // lon_count
    block = features // NB
    mode_share = kept_cols // lat_count
    forward_lon, inverse_lon, lat_cos, lat_sin = mode_tables(
        total_rows, total_cols, kept_rows, kept_cols
    )
    send = jnp.transpose(
        mixer_in.reshape(tile_rows, tile_cols, lon_count, share), (2, 3, 0, 1)
    )
    got = lax.all_to_all(send, "lon", 0, 0, tiled=True)
    along_lon = two_pass(
        "scrw,swn->rcn", got, forward_lon.reshape(lon_count, tile_cols, 2 * kept_cols)
    )
    along_lon = along_lon.reshape(tile_rows, share, 2, lat_count, mode_share)
    outgoing = jnp.transpose(along_lon, (3, 0, 1, 2, 4)).astype(jnp.bfloat16)
    outgoing = outgoing.reshape(lat_count, tile_rows, share * 2 * mode_share)
    columns = lax.all_to_all(outgoing, "lat", 0, 0, tiled=True)
    columns = columns.reshape(total_rows, share * 2 * mode_share)
    lat_table = jnp.concatenate([lat_cos, lat_sin], axis=1)
    both = two_pass("in,it->tn", columns, lat_table)
    both = both.reshape(2, kept_rows, share, 2, mode_share)
    spec_real = both[0, :, :, 0] + both[1, :, :, 1]
    spec_imag = both[0, :, :, 1] - both[1, :, :, 0]
    spectrum = jnp.stack([spec_real, spec_imag])
    lon_index = lax.axis_index("lon")
    half = lon_index % 2
    block_index = lon_index // 2
    pairs = [(i, i ^ 1) for i in range(lon_count)]
    half_rows = kept_rows // 2
    own = lax.dynamic_slice_in_dim(spectrum, half * half_rows, half_rows, axis=1)
    away = lax.dynamic_slice_in_dim(spectrum, (1 - half) * half_rows, half_rows, axis=1)
    came = lax.ppermute(away, "lon", pairs)
    modes = jnp.where(
        half == 0,
        jnp.concatenate([own, came], axis=2),
        jnp.concatenate([came, own], axis=2),
    )
    w1 = lax.dynamic_index_in_dim(first_weight, block_index, axis=1, keepdims=False)
    b1 = lax.dynamic_index_in_dim(first_bias, block_index, axis=1, keepdims=False)
    w2 = lax.dynamic_index_in_dim(second_weight, block_index, axis=1, keepdims=False)
    b2 = lax.dynamic_index_in_dim(second_bias, block_index, axis=1, keepdims=False)
    real_in, imag_in = modes[0], modes[1]
    hidden_r = jax.nn.relu(
        mode_mix(real_in, w1[0]) - mode_mix(imag_in, w1[1]) + b1[0][None, :, None]
    )
    hidden_i = jax.nn.relu(
        mode_mix(imag_in, w1[0]) + mode_mix(real_in, w1[1]) + b1[1][None, :, None]
    )
    filtered_r = mode_mix(hidden_r, w2[0]) - mode_mix(hidden_i, w2[1]) + b2[0][None, :, None]
    filtered_i = mode_mix(hidden_i, w2[0]) + mode_mix(hidden_r, w2[1]) + b2[1][None, :, None]
    filtered = jnp.stack([filtered_r, filtered_i])
    mine = lax.dynamic_slice_in_dim(filtered, half * share, share, axis=2)
    theirs = lax.dynamic_slice_in_dim(filtered, (1 - half) * share, share, axis=2)
    back = lax.ppermute(theirs, "lon", pairs)
    returned = jnp.where(
        half == 0,
        jnp.concatenate([mine, back], axis=1),
        jnp.concatenate([back, mine], axis=1),
    )
    cos_back = jnp.einsum("ik,pkcm->ipcm", lat_cos, returned, precision=THREE_PASS)
    sin_back = jnp.einsum("ik,pkcm->ipcm", lat_sin, returned, precision=THREE_PASS)
    rows_real = cos_back[:, 0] - sin_back[:, 1]
    rows_imag = sin_back[:, 0] + cos_back[:, 1]
    rows = jnp.stack([rows_real, rows_imag], axis=2).astype(jnp.bfloat16)
    rows = rows.reshape(lat_count, tile_rows, share * 2 * mode_share)
    arrived = lax.all_to_all(rows, "lat", 0, 0, tiled=True)
    arrived = arrived.reshape(lat_count, tile_rows, share, 2, mode_share)
    field = two_pass(
        "srcpm,psmj->rcj",
        arrived,
        inverse_lon.reshape(2, lat_count, mode_share, total_cols),
    ).astype(jnp.bfloat16)
    field = jnp.transpose(
        field.reshape(tile_rows, share, lon_count, tile_cols), (2, 0, 3, 1)
    )
    home = lax.all_to_all(field, "lon", 0, 0, tiled=True)
    return lax.optimization_barrier(
        jnp.transpose(home, (1, 2, 0, 3)).reshape(tile_rows, tile_cols, features)
    )


def mode_mix(inputs, weight):
    return jnp.einsum("kcm,co->kom", inputs, weight, precision=HIGHEST)


def solution(mesh):
    placed = (P("lat", "lon", None), P(), P(), P(), P(), P(), P(), P(), P(), P())
    return jax.shard_map(
        shards, mesh=mesh, in_specs=placed, out_specs=P("lat", "lon", None), check_vma=False
    )
```

```python
import functools
import math

import jax
import jax.numpy as jnp
from jax import lax
from jax.sharding import PartitionSpec as P
from jax.experimental import pallas as pl

HEADS = 8
NB = 8
RADIUS = 6


HIGHEST = lax.Precision.HIGHEST
THREE_PASS = lax.Precision.HIGH


def padded_2(cells, sides, width):
    for axis, dim in sides:
        count = lax.axis_size(axis)
        head = lax.slice_in_dim(cells, 0, width, axis=dim)
        tail = lax.slice_in_dim(cells, cells.shape[dim] - width, cells.shape[dim], axis=dim)
        cells = jnp.concatenate(
            [
                lax.ppermute(tail, axis, [(i, (i + 1) % count) for i in range(count)]),
                cells,
                lax.ppermute(head, axis, [((i + 1) % count, i) for i in range(count)]),
            ],
            axis=dim,
        )
    return cells


def normed(values, gain):
    data = values.astype(jnp.float32)
    centre = jnp.mean(data, axis=-1, keepdims=True)
    centred = data - centre
    spread = jnp.mean(centred * centred, axis=-1, keepdims=True)
    return (centred * lax.rsqrt(spread + 1e-05) * gain).astype(jnp.bfloat16)


def mode_tables(total_rows, total_cols, kept_rows, kept_cols):
    factor = 1.0 / math.sqrt(total_rows * total_cols)
    column = jnp.arange(total_cols, dtype=jnp.int32)[:, None]
    lon_freq = jnp.arange(kept_cols, dtype=jnp.int32)[None, :]
    lon_angle = 2.0 * math.pi / total_cols * (column * lon_freq % total_cols).astype(jnp.float32)
    lon_cos = jnp.cos(lon_angle)
    lon_sin = jnp.sin(lon_angle)
    forward_lon = jnp.concatenate([lon_cos, -lon_sin], axis=1) * factor
    doubled = jnp.where(lon_freq == 0, 1.0, 2.0).astype(jnp.float32)
    inverse_lon = (
        jnp.concatenate(
            [jnp.transpose(lon_cos * doubled), jnp.transpose(-lon_sin * doubled)], axis=0
        )
        * factor
    )
    lat_slot = jnp.arange(kept_rows, dtype=jnp.int32)
    lat_freq = lat_slot + jnp.where(lat_slot >= kept_rows // 2, total_rows - kept_rows, 0)
    row_index = jnp.arange(total_rows, dtype=jnp.int32)[:, None]
    lat_angle = (
        2.0
        * math.pi
        / total_rows
        * (row_index * lat_freq[None, :] % total_rows).astype(jnp.float32)
    )
    return (forward_lon, inverse_lon, jnp.cos(lat_angle), jnp.sin(lat_angle))


def block_mix(inputs, weight):
    return jnp.einsum("bim,bio->bom", inputs, weight, precision=HIGHEST)


def shards(
    grid_tokens,
    attention_gain,
    score_weight,
    value_weight,
    output_weight,
    mixer_gain,
    first_weight,
    first_bias,
    second_weight,
    second_bias,
):
    tile_rows, tile_cols, features = grid_tokens.shape
    lat_count = lax.axis_size("lat")
    lon_count = lax.axis_size("lon")
    total_rows = tile_rows * lat_count
    total_cols = tile_cols * lon_count
    head_size = features // HEADS
    span = 2 * RADIUS + 1
    normed_in = normed(grid_tokens, attention_gain)
    flat_in = normed_in.reshape(tile_rows * tile_cols, features)
    queries = jnp.dot(
        flat_in, score_weight[:, :features], preferred_element_type=jnp.float32
    ).astype(jnp.bfloat16)
    queries = queries.reshape(tile_rows, tile_cols, features)
    kv_weight = jnp.concatenate([score_weight[:, features:], value_weight], axis=1)
    projected = jnp.dot(flat_in, kv_weight, preferred_element_type=jnp.float32).astype(jnp.bfloat16)
    projected = projected.reshape(tile_rows, tile_cols, 2 * features)
    padded = padded_2(projected, (("lat", 0), ("lon", 1)), RADIUS)
    key_pad = padded[:, :, :features]
    value_pad = padded[:, :, features:]
    attended = window_attention(queries, key_pad, value_pad, total_rows)
    projected_out = jnp.dot(attended, output_weight, preferred_element_type=jnp.float32)
    after_attention = (
        grid_tokens.astype(jnp.float32).reshape(-1, features) + projected_out
    ).astype(jnp.bfloat16)
    after_attention = after_attention.reshape(tile_rows, tile_cols, features)
    mixer_in = lax.optimization_barrier(normed(after_attention, mixer_gain))
    tile_back = spectral_mix(
        mixer_in, first_weight, first_bias, second_weight, second_bias
    )
    summed = (
        after_attention.astype(jnp.float32)
        + mixer_in.astype(jnp.float32)
        + tile_back.astype(jnp.float32)
    )
    return summed.astype(jnp.bfloat16)


def split_bf16(table):
    high = table.astype(jnp.bfloat16)
    return high, (table - high.astype(jnp.float32)).astype(jnp.bfloat16)


def two_pass(spec, data, table):
    high, rest = split_bf16(table)
    return jnp.einsum(spec, data, high, preferred_element_type=jnp.float32) + jnp.einsum(
        spec, data, rest, preferred_element_type=jnp.float32
    )


def spectral_mix(mixer_in, first_weight, first_bias, second_weight, second_bias):
    tile_rows, tile_cols, features = mixer_in.shape
    lat_count = lax.axis_size("lat")
    lon_count = lax.axis_size("lon")
    total_rows = tile_rows * lat_count
    total_cols = tile_cols * lon_count
    kept_rows = total_rows // 2
    kept_cols = total_cols // 4
    share = features // lon_count
    block = features // NB
    mode_share = kept_cols // lat_count
    forward_lon, inverse_lon, lat_cos, lat_sin = mode_tables(
        total_rows, total_cols, kept_rows, kept_cols
    )
    send = jnp.transpose(
        mixer_in.reshape(tile_rows, tile_cols, lon_count, share), (2, 3, 0, 1)
    )
    got = lax.all_to_all(send, "lon", 0, 0, tiled=True)
    along_lon = two_pass(
        "scrw,swn->rcn", got, forward_lon.reshape(lon_count, tile_cols, 2 * kept_cols)
    )
    along_lon = along_lon.reshape(tile_rows, share, 2, lat_count, mode_share)
    outgoing = jnp.transpose(along_lon, (3, 0, 1, 2, 4)).astype(jnp.bfloat16)
    outgoing = outgoing.reshape(lat_count, tile_rows, share * 2 * mode_share)
    columns = lax.all_to_all(outgoing, "lat", 0, 0, tiled=True)
    columns = columns.reshape(total_rows, share * 2 * mode_share)
    lat_table = jnp.concatenate([lat_cos, lat_sin], axis=1)
    both = two_pass("in,it->tn", columns, lat_table)
    both = both.reshape(2, kept_rows, share, 2, mode_share)
    spec_real = both[0, :, :, 0] + both[1, :, :, 1]
    spec_imag = both[0, :, :, 1] - both[1, :, :, 0]
    spectrum = jnp.stack([spec_real, spec_imag])
    lon_index = lax.axis_index("lon")
    half = lon_index % 2
    block_index = lon_index // 2
    pairs = [(i, i ^ 1) for i in range(lon_count)]
    half_rows = kept_rows // 2
    own = lax.dynamic_slice_in_dim(spectrum, half * half_rows, half_rows, axis=1)
    away = lax.dynamic_slice_in_dim(spectrum, (1 - half) * half_rows, half_rows, axis=1)
    came = lax.ppermute(away, "lon", pairs)
    modes = jnp.where(
        half == 0,
        jnp.concatenate([own, came], axis=2),
        jnp.concatenate([came, own], axis=2),
    )
    w1 = lax.dynamic_index_in_dim(first_weight, block_index, axis=1, keepdims=False)
    b1 = lax.dynamic_index_in_dim(first_bias, block_index, axis=1, keepdims=False)
    w2 = lax.dynamic_index_in_dim(second_weight, block_index, axis=1, keepdims=False)
    b2 = lax.dynamic_index_in_dim(second_bias, block_index, axis=1, keepdims=False)
    real_in, imag_in = modes[0], modes[1]
    hidden_r = jax.nn.relu(
        mode_mix(real_in, w1[0]) - mode_mix(imag_in, w1[1]) + b1[0][None, :, None]
    )
    hidden_i = jax.nn.relu(
        mode_mix(imag_in, w1[0]) + mode_mix(real_in, w1[1]) + b1[1][None, :, None]
    )
    filtered_r = mode_mix(hidden_r, w2[0]) - mode_mix(hidden_i, w2[1]) + b2[0][None, :, None]
    filtered_i = mode_mix(hidden_i, w2[0]) + mode_mix(hidden_r, w2[1]) + b2[1][None, :, None]
    filtered = jnp.stack([filtered_r, filtered_i])
    mine = lax.dynamic_slice_in_dim(filtered, half * share, share, axis=2)
    theirs = lax.dynamic_slice_in_dim(filtered, (1 - half) * share, share, axis=2)
    back = lax.ppermute(theirs, "lon", pairs)
    returned = jnp.where(
        half == 0,
        jnp.concatenate([mine, back], axis=1),
        jnp.concatenate([back, mine], axis=1),
    )
    cos_back = jnp.einsum("ik,pkcm->ipcm", lat_cos, returned, precision=THREE_PASS)
    sin_back = jnp.einsum("ik,pkcm->ipcm", lat_sin, returned, precision=THREE_PASS)
    rows_real = cos_back[:, 0] - sin_back[:, 1]
    rows_imag = sin_back[:, 0] + cos_back[:, 1]
    rows = jnp.stack([rows_real, rows_imag], axis=2).astype(jnp.bfloat16)
    rows = rows.reshape(lat_count, tile_rows, share * 2 * mode_share)
    arrived = lax.all_to_all(rows, "lat", 0, 0, tiled=True)
    arrived = arrived.reshape(lat_count, tile_rows, share, 2, mode_share)
    field = two_pass(
        "srcpm,psmj->rcj",
        arrived,
        inverse_lon.reshape(2, lat_count, mode_share, total_cols),
    ).astype(jnp.bfloat16)
    field = jnp.transpose(
        field.reshape(tile_rows, share, lon_count, tile_cols), (2, 0, 3, 1)
    )
    home = lax.all_to_all(field, "lon", 0, 0, tiled=True)
    return lax.optimization_barrier(
        jnp.transpose(home, (1, 2, 0, 3)).reshape(tile_rows, tile_cols, features)
    )


def mode_mix(inputs, weight):
    return jnp.einsum("kcm,co->kom", inputs, weight, precision=HIGHEST)


def attention_kernel(q_ref, k_ref, v_ref, bias_ref, o_ref, *, step, length, scale):
    start = pl.multiple_of(pl.program_id(0) * step, 8)
    q = q_ref[...]
    k = k_ref[pl.ds(start, length), :]
    v = v_ref[pl.ds(start, length), :]
    bias = bias_ref[...]
    first = lax.broadcasted_iota(jnp.int32, q.shape, 1) < q.shape[1] // 2
    results = []
    for lanes in (first, jnp.logical_not(first)):
        head_q = jnp.where(lanes, q, jnp.zeros_like(q))
        scores = (
            lax.dot_general(
                head_q, k, (((1,), (1,)), ((), ())), preferred_element_type=jnp.float32
            )
            * scale
            + bias
        )
        largest = jnp.max(scores, axis=1, keepdims=True)
        weights = jnp.exp(scores - largest)
        probs = (weights / jnp.sum(weights, axis=1, keepdims=True)).astype(jnp.bfloat16)
        results.append(jnp.dot(probs, v, preferred_element_type=jnp.float32))
    o_ref[...] = jnp.where(first, results[0], results[1]).astype(o_ref.dtype)


def window_attention(queries, key_pad, value_pad, total_rows):
    tile_rows, tile_cols, features = queries.shape
    span = 2 * RADIUS + 1
    block_rows = 12
    block_cols = tile_cols // 2
    row_blocks = tile_rows // block_rows
    col_blocks = tile_cols // block_cols
    key_rows = block_rows + 2 * RADIUS
    key_cols = block_cols + 2 * RADIUS
    slab_cols = -(-key_cols // 8) * 8
    pad_rows = key_pad.shape[0]
    lanes = 128
    head_size = features // HEADS
    block_q = block_rows * block_cols
    block_k = key_rows * slab_cols
    query_blocks = jnp.transpose(
        queries.reshape(row_blocks, block_rows, col_blocks, block_cols, features), (2, 0, 1, 3, 4)
    ).reshape(col_blocks, row_blocks * block_q, features)

    def slabs(table):
        pieces = [
            table[:, c * block_cols : c * block_cols + key_cols] for c in range(col_blocks)
        ]
        stacked = jnp.stack(pieces)
        stacked = jnp.pad(stacked, ((0, 0), (0, 0), (0, slab_cols - key_cols), (0, 0)))
        return stacked.reshape(col_blocks, pad_rows * slab_cols, features)

    key_slabs = slabs(key_pad)
    value_slabs = slabs(value_pad)
    row_anchor = lax.axis_index("lat") * tile_rows
    query_rows = row_anchor + jnp.arange(tile_rows, dtype=jnp.int32).reshape(row_blocks, block_rows)
    window_start = jnp.clip(query_rows - RADIUS, 0, total_rows - span)
    global_key_rows = (
        row_anchor
        - RADIUS
        + block_rows * jnp.arange(row_blocks, dtype=jnp.int32)[:, None]
        + jnp.arange(key_rows, dtype=jnp.int32)[None, :]
    )
    row_inside = (global_key_rows[:, None, :] >= window_start[:, :, None]) & (
        global_key_rows[:, None, :] < window_start[:, :, None] + span
    )
    column_gap = (
        jnp.arange(slab_cols, dtype=jnp.int32)[None, :]
        - jnp.arange(block_cols, dtype=jnp.int32)[:, None]
    )
    column_inside = (column_gap >= 0) & (column_gap < span)
    allowed = row_inside[:, :, None, :, None] & column_inside[None, None, :, None, :]
    bias = jnp.where(allowed, 0.0, -1e30).astype(jnp.float32)
    bias = bias.reshape(row_blocks, block_q, block_k)
    kernel = functools.partial(
        attention_kernel,
        step=block_rows * slab_cols,
        length=block_k,
        scale=1.0 / math.sqrt(head_size),
    )
    pairs = features // lanes
    flops = 2 * 2 * 2 * block_q * block_k * lanes * row_blocks * col_blocks * pairs
    out = pl.pallas_call(
        kernel,
        out_shape=jax.ShapeDtypeStruct(query_blocks.shape, jnp.bfloat16),
        grid=(row_blocks, col_blocks, pairs),
        in_specs=[
            pl.BlockSpec((None, block_q, lanes), lambda r, c, h: (c, r, h)),
            pl.BlockSpec((None, pad_rows * slab_cols, lanes), lambda r, c, h: (c, 0, h)),
            pl.BlockSpec((None, pad_rows * slab_cols, lanes), lambda r, c, h: (c, 0, h)),
            pl.BlockSpec((None, block_q, block_k), lambda r, c, h: (r, 0, 0)),
        ],
        out_specs=pl.BlockSpec((None, block_q, lanes), lambda r, c, h: (c, r, h)),
        cost_estimate=pl.CostEstimate(
            flops=flops,
            transcendentals=2 * block_q * block_k * row_blocks * col_blocks * pairs,
            bytes_accessed=2 * (query_blocks.size * 2 + key_slabs.size * 2 * 2) + bias.size * 4,
        ),
    )(query_blocks, key_slabs, value_slabs, bias)
    out = jnp.transpose(
        out.reshape(col_blocks, row_blocks, block_rows, block_cols, features), (1, 2, 0, 3, 4)
    )
    return out.reshape(tile_rows * tile_cols, features)


def solution(mesh):
    placed = (P("lat", "lon", None), P(), P(), P(), P(), P(), P(), P(), P(), P())
    return jax.shard_map(
        shards, mesh=mesh, in_specs=placed, out_specs=P("lat", "lon", None), check_vma=False
    )
```

```python
import functools
import math

import jax
import jax.numpy as jnp
from jax import lax
from jax.sharding import PartitionSpec as P
from jax.experimental import pallas as pl

HEADS = 8
NB = 8
RADIUS = 6


HIGHEST = lax.Precision.HIGHEST
THREE_PASS = lax.Precision.HIGH


def padded_2(cells, sides, width):
    for axis, dim in sides:
        count = lax.axis_size(axis)
        head = lax.slice_in_dim(cells, 0, width, axis=dim)
        tail = lax.slice_in_dim(cells, cells.shape[dim] - width, cells.shape[dim], axis=dim)
        cells = jnp.concatenate(
            [
                lax.ppermute(tail, axis, [(i, (i + 1) % count) for i in range(count)]),
                cells,
                lax.ppermute(head, axis, [((i + 1) % count, i) for i in range(count)]),
            ],
            axis=dim,
        )
    return cells


def normed(values, gain):
    data = values.astype(jnp.float32)
    centre = jnp.mean(data, axis=-1, keepdims=True)
    centred = data - centre
    spread = jnp.mean(centred * centred, axis=-1, keepdims=True)
    return (centred * lax.rsqrt(spread + 1e-05) * gain).astype(jnp.bfloat16)


def mode_tables(total_rows, total_cols, kept_rows, kept_cols):
    factor = 1.0 / math.sqrt(total_rows * total_cols)
    column = jnp.arange(total_cols, dtype=jnp.int32)[:, None]
    lon_freq = jnp.arange(kept_cols, dtype=jnp.int32)[None, :]
    lon_angle = 2.0 * math.pi / total_cols * (column * lon_freq % total_cols).astype(jnp.float32)
    lon_cos = jnp.cos(lon_angle)
    lon_sin = jnp.sin(lon_angle)
    forward_lon = jnp.concatenate([lon_cos, -lon_sin], axis=1) * factor
    doubled = jnp.where(lon_freq == 0, 1.0, 2.0).astype(jnp.float32)
    inverse_lon = (
        jnp.concatenate(
            [jnp.transpose(lon_cos * doubled), jnp.transpose(-lon_sin * doubled)], axis=0
        )
        * factor
    )
    lat_slot = jnp.arange(kept_rows, dtype=jnp.int32)
    lat_freq = lat_slot + jnp.where(lat_slot >= kept_rows // 2, total_rows - kept_rows, 0)
    row_index = jnp.arange(total_rows, dtype=jnp.int32)[:, None]
    lat_angle = (
        2.0
        * math.pi
        / total_rows
        * (row_index * lat_freq[None, :] % total_rows).astype(jnp.float32)
    )
    return (forward_lon, inverse_lon, jnp.cos(lat_angle), jnp.sin(lat_angle))


def block_mix(inputs, weight):
    return jnp.einsum("bim,bio->bom", inputs, weight, precision=HIGHEST)


def shards(
    grid_tokens,
    attention_gain,
    score_weight,
    value_weight,
    output_weight,
    mixer_gain,
    first_weight,
    first_bias,
    second_weight,
    second_bias,
):
    tile_rows, tile_cols, features = grid_tokens.shape
    lat_count = lax.axis_size("lat")
    lon_count = lax.axis_size("lon")
    total_rows = tile_rows * lat_count
    total_cols = tile_cols * lon_count
    head_size = features // HEADS
    span = 2 * RADIUS + 1
    normed_in = normed(grid_tokens, attention_gain)
    flat_in = normed_in.reshape(tile_rows * tile_cols, features)
    queries = jnp.dot(
        flat_in, score_weight[:, :features], preferred_element_type=jnp.float32
    ).astype(jnp.bfloat16)
    queries = queries.reshape(tile_rows, tile_cols, features)
    kv_weight = jnp.concatenate([score_weight[:, features:], value_weight], axis=1)
    projected = jnp.dot(flat_in, kv_weight, preferred_element_type=jnp.float32).astype(jnp.bfloat16)
    projected = projected.reshape(tile_rows, tile_cols, 2 * features)
    padded = padded_2(projected, (("lat", 0), ("lon", 1)), RADIUS)
    key_pad = padded[:, :, :features]
    value_pad = padded[:, :, features:]
    attended = window_attention(queries, key_pad, value_pad, total_rows)
    projected_out = jnp.dot(attended, output_weight, preferred_element_type=jnp.float32)
    after_attention = (
        grid_tokens.astype(jnp.float32).reshape(-1, features) + projected_out
    ).astype(jnp.bfloat16)
    after_attention = after_attention.reshape(tile_rows, tile_cols, features)
    mixer_in = lax.optimization_barrier(normed(after_attention, mixer_gain))
    tile_back = spectral_mix(
        mixer_in, first_weight, first_bias, second_weight, second_bias
    )
    summed = (
        after_attention.astype(jnp.float32)
        + mixer_in.astype(jnp.float32)
        + tile_back.astype(jnp.float32)
    )
    return summed.astype(jnp.bfloat16)


def split_bf16(table):
    high = table.astype(jnp.bfloat16)
    return high, (table - high.astype(jnp.float32)).astype(jnp.bfloat16)


def two_pass(spec, data, table):
    high, rest = split_bf16(table)
    return jnp.einsum(spec, data, high, preferred_element_type=jnp.float32) + jnp.einsum(
        spec, data, rest, preferred_element_type=jnp.float32
    )


def spectral_mix(mixer_in, first_weight, first_bias, second_weight, second_bias):
    tile_rows, tile_cols, features = mixer_in.shape
    lat_count = lax.axis_size("lat")
    lon_count = lax.axis_size("lon")
    total_rows = tile_rows * lat_count
    total_cols = tile_cols * lon_count
    kept_rows = total_rows // 2
    kept_cols = total_cols // 4
    share = features // lon_count
    block = features // NB
    mode_share = kept_cols // lat_count
    forward_lon, inverse_lon, lat_cos, lat_sin = mode_tables(
        total_rows, total_cols, kept_rows, kept_cols
    )
    send = regroup(mixer_in, lon_count)
    got = lax.all_to_all(send, "lon", 0, 0, tiled=True)
    along = two_pass(
        "jf,jn->nf", got.reshape(total_cols, tile_rows * share), forward_lon
    )
    along_lon = jnp.transpose(
        along.reshape(2, lat_count, mode_share, tile_rows, share), (3, 4, 0, 1, 2)
    )
    outgoing = jnp.transpose(along_lon, (3, 0, 1, 2, 4)).astype(jnp.bfloat16)
    outgoing = outgoing.reshape(lat_count, tile_rows, share * 2 * mode_share)
    columns = lax.all_to_all(outgoing, "lat", 0, 0, tiled=True)
    columns = columns.reshape(total_rows, share * 2 * mode_share)
    lat_table = jnp.concatenate([lat_cos, lat_sin], axis=1)
    both = two_pass("in,it->tn", columns, lat_table)
    both = both.reshape(2, kept_rows, share, 2, mode_share)
    spec_real = both[0, :, :, 0] + both[1, :, :, 1]
    spec_imag = both[0, :, :, 1] - both[1, :, :, 0]
    spectrum = jnp.stack([spec_real, spec_imag])
    lon_index = lax.axis_index("lon")
    half = lon_index % 2
    block_index = lon_index // 2
    pairs = [(i, i ^ 1) for i in range(lon_count)]
    half_rows = kept_rows // 2
    own = lax.dynamic_slice_in_dim(spectrum, half * half_rows, half_rows, axis=1)
    away = lax.dynamic_slice_in_dim(spectrum, (1 - half) * half_rows, half_rows, axis=1)
    came = lax.ppermute(away, "lon", pairs)
    modes = jnp.where(
        half == 0,
        jnp.concatenate([own, came], axis=2),
        jnp.concatenate([came, own], axis=2),
    )
    w1 = lax.dynamic_index_in_dim(first_weight, block_index, axis=1, keepdims=False)
    b1 = lax.dynamic_index_in_dim(first_bias, block_index, axis=1, keepdims=False)
    w2 = lax.dynamic_index_in_dim(second_weight, block_index, axis=1, keepdims=False)
    b2 = lax.dynamic_index_in_dim(second_bias, block_index, axis=1, keepdims=False)
    real_in, imag_in = modes[0], modes[1]
    hidden_r = jax.nn.relu(
        mode_mix(real_in, w1[0]) - mode_mix(imag_in, w1[1]) + b1[0][None, :, None]
    )
    hidden_i = jax.nn.relu(
        mode_mix(imag_in, w1[0]) + mode_mix(real_in, w1[1]) + b1[1][None, :, None]
    )
    filtered_r = mode_mix(hidden_r, w2[0]) - mode_mix(hidden_i, w2[1]) + b2[0][None, :, None]
    filtered_i = mode_mix(hidden_i, w2[0]) + mode_mix(hidden_r, w2[1]) + b2[1][None, :, None]
    filtered = jnp.stack([filtered_r, filtered_i])
    mine = lax.dynamic_slice_in_dim(filtered, half * share, share, axis=2)
    theirs = lax.dynamic_slice_in_dim(filtered, (1 - half) * share, share, axis=2)
    back = lax.ppermute(theirs, "lon", pairs)
    returned = jnp.where(
        half == 0,
        jnp.concatenate([mine, back], axis=1),
        jnp.concatenate([back, mine], axis=1),
    )
    cos_back = jnp.einsum("ik,pkcm->ipcm", lat_cos, returned, precision=THREE_PASS)
    sin_back = jnp.einsum("ik,pkcm->ipcm", lat_sin, returned, precision=THREE_PASS)
    rows_real = cos_back[:, 0] - sin_back[:, 1]
    rows_imag = sin_back[:, 0] + cos_back[:, 1]
    rows = jnp.stack([rows_real, rows_imag], axis=2).astype(jnp.bfloat16)
    rows = rows.reshape(lat_count, tile_rows, share * 2 * mode_share)
    arrived = lax.all_to_all(rows, "lat", 0, 0, tiled=True)
    arrived = arrived.reshape(lat_count, tile_rows, share, 2, mode_share)
    by_mode = jnp.transpose(arrived, (3, 0, 4, 1, 2)).reshape(2 * kept_cols, tile_rows * share)
    field = two_pass("nf,nj->jf", by_mode, inverse_lon).astype(jnp.bfloat16)
    home = lax.all_to_all(
        field.reshape(lon_count, tile_cols, tile_rows * share), "lon", 0, 0, tiled=True
    )
    return ungroup(home, tile_rows)


def regroup_kernel(x_ref, y_ref):
    rows = x_ref.shape[0]
    groups, _, width = y_ref.shape
    share = width // rows
    for g in range(groups):
        for r in range(rows):
            y_ref[g, :, r * share : (r + 1) * share] = x_ref[r, :, g * share : (g + 1) * share]


def ungroup_kernel(y_ref, x_ref):
    rows = x_ref.shape[0]
    groups, _, width = y_ref.shape
    share = width // rows
    for g in range(groups):
        for r in range(rows):
            x_ref[r, :, g * share : (g + 1) * share] = y_ref[g, :, r * share : (r + 1) * share]


def regroup(tile, groups):
    rows, cols, features = tile.shape
    return pl.pallas_call(
        regroup_kernel,
        out_shape=jax.ShapeDtypeStruct((groups, cols, rows * features // groups), tile.dtype),
        cost_estimate=pl.CostEstimate(flops=0, transcendentals=0, bytes_accessed=2 * tile.size * 2),
    )(tile)


def ungroup(grouped, rows):
    groups, cols, width = grouped.shape
    return pl.pallas_call(
        ungroup_kernel,
        out_shape=jax.ShapeDtypeStruct((rows, cols, groups * width // rows), grouped.dtype),
        cost_estimate=pl.CostEstimate(flops=0, transcendentals=0, bytes_accessed=2 * grouped.size * 2),
    )(grouped)

def mode_mix(inputs, weight):
    return jnp.einsum("kcm,co->kom", inputs, weight, precision=HIGHEST)


def attention_kernel(q_ref, k_ref, v_ref, bias_ref, o_ref, *, step, length, scale):
    start = pl.multiple_of(pl.program_id(0) * step, 8)
    q = q_ref[...]
    k = k_ref[pl.ds(start, length), :]
    v = v_ref[pl.ds(start, length), :]
    bias = bias_ref[...]
    first = lax.broadcasted_iota(jnp.int32, q.shape, 1) < q.shape[1] // 2
    results = []
    for lanes in (first, jnp.logical_not(first)):
        head_q = jnp.where(lanes, q, jnp.zeros_like(q))
        scores = (
            lax.dot_general(
                head_q, k, (((1,), (1,)), ((), ())), preferred_element_type=jnp.float32
            )
            * scale
            + bias
        )
        largest = jnp.max(scores, axis=1, keepdims=True)
        weights = jnp.exp(scores - largest)
        probs = (weights / jnp.sum(weights, axis=1, keepdims=True)).astype(jnp.bfloat16)
        results.append(jnp.dot(probs, v, preferred_element_type=jnp.float32))
    o_ref[...] = jnp.where(first, results[0], results[1]).astype(o_ref.dtype)


def window_attention(queries, key_pad, value_pad, total_rows):
    tile_rows, tile_cols, features = queries.shape
    span = 2 * RADIUS + 1
    block_rows = 12
    block_cols = tile_cols // 2
    row_blocks = tile_rows // block_rows
    col_blocks = tile_cols // block_cols
    key_rows = block_rows + 2 * RADIUS
    key_cols = block_cols + 2 * RADIUS
    slab_cols = -(-key_cols // 8) * 8
    pad_rows = key_pad.shape[0]
    lanes = 128
    head_size = features // HEADS
    block_q = block_rows * block_cols
    block_k = key_rows * slab_cols
    query_blocks = jnp.transpose(
        queries.reshape(row_blocks, block_rows, col_blocks, block_cols, features), (2, 0, 1, 3, 4)
    ).reshape(col_blocks, row_blocks * block_q, features)

    def slabs(table):
        pieces = [
            table[:, c * block_cols : c * block_cols + key_cols] for c in range(col_blocks)
        ]
        stacked = jnp.stack(pieces)
        stacked = jnp.pad(stacked, ((0, 0), (0, 0), (0, slab_cols - key_cols), (0, 0)))
        return stacked.reshape(col_blocks, pad_rows * slab_cols, features)

    key_slabs = slabs(key_pad)
    value_slabs = slabs(value_pad)
    row_anchor = lax.axis_index("lat") * tile_rows
    query_rows = row_anchor + jnp.arange(tile_rows, dtype=jnp.int32).reshape(row_blocks, block_rows)
    window_start = jnp.clip(query_rows - RADIUS, 0, total_rows - span)
    global_key_rows = (
        row_anchor
        - RADIUS
        + block_rows * jnp.arange(row_blocks, dtype=jnp.int32)[:, None]
        + jnp.arange(key_rows, dtype=jnp.int32)[None, :]
    )
    row_inside = (global_key_rows[:, None, :] >= window_start[:, :, None]) & (
        global_key_rows[:, None, :] < window_start[:, :, None] + span
    )
    column_gap = (
        jnp.arange(slab_cols, dtype=jnp.int32)[None, :]
        - jnp.arange(block_cols, dtype=jnp.int32)[:, None]
    )
    column_inside = (column_gap >= 0) & (column_gap < span)
    allowed = row_inside[:, :, None, :, None] & column_inside[None, None, :, None, :]
    bias = jnp.where(allowed, 0.0, -1e30).astype(jnp.float32)
    bias = bias.reshape(row_blocks, block_q, block_k)
    kernel = functools.partial(
        attention_kernel,
        step=block_rows * slab_cols,
        length=block_k,
        scale=1.0 / math.sqrt(head_size),
    )
    pairs = features // lanes
    flops = 2 * 2 * 2 * block_q * block_k * lanes * row_blocks * col_blocks * pairs
    out = pl.pallas_call(
        kernel,
        out_shape=jax.ShapeDtypeStruct(query_blocks.shape, jnp.bfloat16),
        grid=(row_blocks, col_blocks, pairs),
        in_specs=[
            pl.BlockSpec((None, block_q, lanes), lambda r, c, h: (c, r, h)),
            pl.BlockSpec((None, pad_rows * slab_cols, lanes), lambda r, c, h: (c, 0, h)),
            pl.BlockSpec((None, pad_rows * slab_cols, lanes), lambda r, c, h: (c, 0, h)),
            pl.BlockSpec((None, block_q, block_k), lambda r, c, h: (r, 0, 0)),
        ],
        out_specs=pl.BlockSpec((None, block_q, lanes), lambda r, c, h: (c, r, h)),
        cost_estimate=pl.CostEstimate(
            flops=flops,
            transcendentals=2 * block_q * block_k * row_blocks * col_blocks * pairs,
            bytes_accessed=2 * (query_blocks.size * 2 + key_slabs.size * 2 * 2) + bias.size * 4,
        ),
    )(query_blocks, key_slabs, value_slabs, bias)
    out = jnp.transpose(
        out.reshape(col_blocks, row_blocks, block_rows, block_cols, features), (1, 2, 0, 3, 4)
    )
    return out.reshape(tile_rows * tile_cols, features)


def solution(mesh):
    placed = (P("lat", "lon", None), P(), P(), P(), P(), P(), P(), P(), P(), P())
    return jax.shard_map(
        shards, mesh=mesh, in_specs=placed, out_specs=P("lat", "lon", None), check_vma=False
    )
```

```python
import functools
import math

import jax
import jax.numpy as jnp
from jax import lax
from jax.sharding import PartitionSpec as P
from jax.experimental import pallas as pl

HEADS = 8
NB = 8
RADIUS = 6


HIGHEST = lax.Precision.HIGHEST
THREE_PASS = lax.Precision.HIGH


def padded_2(cells, sides, width):
    for axis, dim in sides:
        count = lax.axis_size(axis)
        head = lax.slice_in_dim(cells, 0, width, axis=dim)
        tail = lax.slice_in_dim(cells, cells.shape[dim] - width, cells.shape[dim], axis=dim)
        cells = jnp.concatenate(
            [
                lax.ppermute(tail, axis, [(i, (i + 1) % count) for i in range(count)]),
                cells,
                lax.ppermute(head, axis, [((i + 1) % count, i) for i in range(count)]),
            ],
            axis=dim,
        )
    return cells


def normed(values, gain):
    data = values.astype(jnp.float32)
    centre = jnp.mean(data, axis=-1, keepdims=True)
    centred = data - centre
    spread = jnp.mean(centred * centred, axis=-1, keepdims=True)
    return (centred * lax.rsqrt(spread + 1e-05) * gain).astype(jnp.bfloat16)


def mode_tables(total_rows, total_cols, kept_rows, kept_cols):
    factor = 1.0 / math.sqrt(total_rows * total_cols)
    column = jnp.arange(total_cols, dtype=jnp.int32)[:, None]
    lon_freq = jnp.arange(kept_cols, dtype=jnp.int32)[None, :]
    lon_angle = 2.0 * math.pi / total_cols * (column * lon_freq % total_cols).astype(jnp.float32)
    lon_cos = jnp.cos(lon_angle)
    lon_sin = jnp.sin(lon_angle)
    forward_lon = jnp.concatenate([lon_cos, -lon_sin], axis=1) * factor
    doubled = jnp.where(lon_freq == 0, 1.0, 2.0).astype(jnp.float32)
    inverse_lon = (
        jnp.concatenate(
            [jnp.transpose(lon_cos * doubled), jnp.transpose(-lon_sin * doubled)], axis=0
        )
        * factor
    )
    lat_slot = jnp.arange(kept_rows, dtype=jnp.int32)
    lat_freq = lat_slot + jnp.where(lat_slot >= kept_rows // 2, total_rows - kept_rows, 0)
    row_index = jnp.arange(total_rows, dtype=jnp.int32)[:, None]
    lat_angle = (
        2.0
        * math.pi
        / total_rows
        * (row_index * lat_freq[None, :] % total_rows).astype(jnp.float32)
    )
    return (forward_lon, inverse_lon, jnp.cos(lat_angle), jnp.sin(lat_angle))


def block_mix(inputs, weight):
    return jnp.einsum("bim,bio->bom", inputs, weight, precision=HIGHEST)


def shards(
    grid_tokens,
    attention_gain,
    score_weight,
    value_weight,
    output_weight,
    mixer_gain,
    first_weight,
    first_bias,
    second_weight,
    second_bias,
):
    tile_rows, tile_cols, features = grid_tokens.shape
    lat_count = lax.axis_size("lat")
    lon_count = lax.axis_size("lon")
    total_rows = tile_rows * lat_count
    total_cols = tile_cols * lon_count
    head_size = features // HEADS
    span = 2 * RADIUS + 1
    normed_in = normed(grid_tokens, attention_gain)
    flat_in = normed_in.reshape(tile_rows * tile_cols, features)
    queries = jnp.dot(
        flat_in, score_weight[:, :features], preferred_element_type=jnp.float32
    ).astype(jnp.bfloat16)
    queries = queries.reshape(tile_rows, tile_cols, features)
    kv_weight = jnp.concatenate([score_weight[:, features:], value_weight], axis=1)
    projected = jnp.dot(flat_in, kv_weight, preferred_element_type=jnp.float32).astype(jnp.bfloat16)
    projected = projected.reshape(tile_rows, tile_cols, 2 * features)
    padded = padded_2(projected, (("lat", 0), ("lon", 1)), RADIUS)
    key_pad = padded[:, :, :features]
    value_pad = padded[:, :, features:]
    attended = window_attention(queries, key_pad, value_pad, total_rows)
    projected_out = jnp.dot(attended, output_weight, preferred_element_type=jnp.float32)
    after_attention = (
        grid_tokens.astype(jnp.float32).reshape(-1, features) + projected_out
    ).astype(jnp.bfloat16)
    after_attention = after_attention.reshape(tile_rows, tile_cols, features)
    mixer_in = lax.optimization_barrier(normed(after_attention, mixer_gain))
    tile_back = spectral_mix(
        mixer_in, first_weight, first_bias, second_weight, second_bias
    )
    summed = (
        after_attention.astype(jnp.float32)
        + mixer_in.astype(jnp.float32)
        + tile_back.astype(jnp.float32)
    )
    return summed.astype(jnp.bfloat16)


def split_bf16(table):
    high = table.astype(jnp.bfloat16)
    return high, (table - high.astype(jnp.float32)).astype(jnp.bfloat16)


def two_pass(spec, data, table):
    high, rest = split_bf16(table)
    return jnp.einsum(spec, data, high, preferred_element_type=jnp.float32) + jnp.einsum(
        spec, data, rest, preferred_element_type=jnp.float32
    )


def spectral_mix(mixer_in, first_weight, first_bias, second_weight, second_bias):
    tile_rows, tile_cols, features = mixer_in.shape
    lat_count = lax.axis_size("lat")
    lon_count = lax.axis_size("lon")
    total_rows = tile_rows * lat_count
    total_cols = tile_cols * lon_count
    kept_rows = total_rows // 2
    kept_cols = total_cols // 4
    share = features // lon_count
    block = features // NB
    mode_share = kept_cols // lat_count
    forward_lon, inverse_lon, lat_cos, lat_sin = mode_tables(
        total_rows, total_cols, kept_rows, kept_cols
    )
    forward_lon = jnp.transpose(
        forward_lon.reshape(total_cols, 2, lat_count, mode_share), (0, 2, 1, 3)
    ).reshape(total_cols, 2 * kept_cols)
    inverse_lon = jnp.transpose(
        inverse_lon.reshape(2, lat_count, mode_share, total_cols), (1, 0, 2, 3)
    ).reshape(2 * kept_cols, total_cols)
    send = regroup(mixer_in, lon_count)
    got = lax.all_to_all(send, "lon", 0, 0, tiled=True)
    along = two_pass(
        "jf,jn->nf", got.reshape(total_cols, tile_rows * share), forward_lon
    )
    outgoing = along.astype(jnp.bfloat16).reshape(lat_count, 2 * mode_share, tile_rows * share)
    columns = lax.all_to_all(outgoing, "lat", 0, 0, tiled=True)
    columns = columns.reshape(lat_count, 2 * mode_share, tile_rows, share)
    lat_table = jnp.concatenate([lat_cos, lat_sin], axis=1).reshape(
        lat_count, tile_rows, 2 * kept_rows
    )
    both = two_pass("sqrc,srt->tqc", columns, lat_table)
    both = both.reshape(2, kept_rows, 2, mode_share, share)
    spec_real = both[0, :, 0] + both[1, :, 1]
    spec_imag = both[0, :, 1] - both[1, :, 0]
    spectrum = jnp.stack([spec_real, spec_imag])
    lon_index = lax.axis_index("lon")
    half = lon_index % 2
    block_index = lon_index // 2
    pairs = [(i, i ^ 1) for i in range(lon_count)]
    half_rows = kept_rows // 2
    own = lax.dynamic_slice_in_dim(spectrum, half * half_rows, half_rows, axis=1)
    away = lax.dynamic_slice_in_dim(spectrum, (1 - half) * half_rows, half_rows, axis=1)
    came = lax.ppermute(away, "lon", pairs)
    modes = jnp.where(
        half == 0,
        jnp.concatenate([own, came], axis=3),
        jnp.concatenate([came, own], axis=3),
    )
    w1 = lax.dynamic_index_in_dim(first_weight, block_index, axis=1, keepdims=False)
    b1 = lax.dynamic_index_in_dim(first_bias, block_index, axis=1, keepdims=False)
    w2 = lax.dynamic_index_in_dim(second_weight, block_index, axis=1, keepdims=False)
    b2 = lax.dynamic_index_in_dim(second_bias, block_index, axis=1, keepdims=False)
    real_in, imag_in = modes[0], modes[1]
    hidden_r = jax.nn.relu(mode_mix(real_in, w1[0]) - mode_mix(imag_in, w1[1]) + b1[0])
    hidden_i = jax.nn.relu(mode_mix(imag_in, w1[0]) + mode_mix(real_in, w1[1]) + b1[1])
    filtered_r = mode_mix(hidden_r, w2[0]) - mode_mix(hidden_i, w2[1]) + b2[0]
    filtered_i = mode_mix(hidden_i, w2[0]) + mode_mix(hidden_r, w2[1]) + b2[1]
    filtered = jnp.stack([filtered_r, filtered_i])
    mine = lax.dynamic_slice_in_dim(filtered, half * share, share, axis=3)
    theirs = lax.dynamic_slice_in_dim(filtered, (1 - half) * share, share, axis=3)
    back = lax.ppermute(theirs, "lon", pairs)
    returned = jnp.where(
        half == 0,
        jnp.concatenate([mine, back], axis=1),
        jnp.concatenate([back, mine], axis=1),
    )
    row_cos = lat_cos.reshape(lat_count, tile_rows, kept_rows)
    row_sin = lat_sin.reshape(lat_count, tile_rows, kept_rows)
    cos_back = jnp.einsum("ark,pkmc->apmrc", row_cos, returned, precision=THREE_PASS)
    sin_back = jnp.einsum("ark,pkmc->apmrc", row_sin, returned, precision=THREE_PASS)
    rows_real = cos_back[:, 0] - sin_back[:, 1]
    rows_imag = sin_back[:, 0] + cos_back[:, 1]
    rows = jnp.stack([rows_real, rows_imag], axis=1).astype(jnp.bfloat16)
    rows = rows.reshape(lat_count, 2 * mode_share, tile_rows * share)
    arrived = lax.all_to_all(rows, "lat", 0, 0, tiled=True)
    by_mode = arrived.reshape(2 * kept_cols, tile_rows * share)
    field = two_pass("nf,nj->jf", by_mode, inverse_lon).astype(jnp.bfloat16)
    home = lax.all_to_all(
        field.reshape(lon_count, tile_cols, tile_rows * share), "lon", 0, 0, tiled=True
    )
    return ungroup(home, tile_rows)


def regroup_kernel(x_ref, y_ref):
    rows = x_ref.shape[0]
    groups, _, width = y_ref.shape
    share = width // rows
    for g in range(groups):
        for r in range(rows):
            y_ref[g, :, r * share : (r + 1) * share] = x_ref[r, :, g * share : (g + 1) * share]


def ungroup_kernel(y_ref, x_ref):
    rows = x_ref.shape[0]
    groups, _, width = y_ref.shape
    share = width // rows
    for g in range(groups):
        for r in range(rows):
            x_ref[r, :, g * share : (g + 1) * share] = y_ref[g, :, r * share : (r + 1) * share]


def regroup(tile, groups):
    rows, cols, features = tile.shape
    return pl.pallas_call(
        regroup_kernel,
        out_shape=jax.ShapeDtypeStruct((groups, cols, rows * features // groups), tile.dtype),
        cost_estimate=pl.CostEstimate(flops=0, transcendentals=0, bytes_accessed=2 * tile.size * 2),
    )(tile)


def ungroup(grouped, rows):
    groups, cols, width = grouped.shape
    return pl.pallas_call(
        ungroup_kernel,
        out_shape=jax.ShapeDtypeStruct((rows, cols, groups * width // rows), grouped.dtype),
        cost_estimate=pl.CostEstimate(flops=0, transcendentals=0, bytes_accessed=2 * grouped.size * 2),
    )(grouped)

def mode_mix(inputs, weight):
    return jnp.einsum("kmc,co->kmo", inputs, weight, precision=HIGHEST)


def attention_kernel(q_ref, k_ref, v_ref, bias_ref, o_ref, *, step, length, scale):
    start = pl.multiple_of(pl.program_id(0) * step, 8)
    q = q_ref[...]
    k = k_ref[pl.ds(start, length), :]
    v = v_ref[pl.ds(start, length), :]
    bias = bias_ref[...]
    first = lax.broadcasted_iota(jnp.int32, q.shape, 1) < q.shape[1] // 2
    results = []
    for lanes in (first, jnp.logical_not(first)):
        head_q = jnp.where(lanes, q, jnp.zeros_like(q))
        scores = (
            lax.dot_general(
                head_q, k, (((1,), (1,)), ((), ())), preferred_element_type=jnp.float32
            )
            * scale
            + bias
        )
        largest = jnp.max(scores, axis=1, keepdims=True)
        weights = jnp.exp(scores - largest)
        probs = (weights / jnp.sum(weights, axis=1, keepdims=True)).astype(jnp.bfloat16)
        results.append(jnp.dot(probs, v, preferred_element_type=jnp.float32))
    o_ref[...] = jnp.where(first, results[0], results[1]).astype(o_ref.dtype)


def window_attention(queries, key_pad, value_pad, total_rows):
    tile_rows, tile_cols, features = queries.shape
    span = 2 * RADIUS + 1
    block_rows = 12
    block_cols = tile_cols // 2
    row_blocks = tile_rows // block_rows
    col_blocks = tile_cols // block_cols
    key_rows = block_rows + 2 * RADIUS
    key_cols = block_cols + 2 * RADIUS
    slab_cols = -(-key_cols // 8) * 8
    pad_rows = key_pad.shape[0]
    lanes = 128
    head_size = features // HEADS
    block_q = block_rows * block_cols
    block_k = key_rows * slab_cols
    query_blocks = jnp.transpose(
        queries.reshape(row_blocks, block_rows, col_blocks, block_cols, features), (2, 0, 1, 3, 4)
    ).reshape(col_blocks, row_blocks * block_q, features)

    def slabs(table):
        pieces = [
            table[:, c * block_cols : c * block_cols + key_cols] for c in range(col_blocks)
        ]
        stacked = jnp.stack(pieces)
        stacked = jnp.pad(stacked, ((0, 0), (0, 0), (0, slab_cols - key_cols), (0, 0)))
        return stacked.reshape(col_blocks, pad_rows * slab_cols, features)

    key_slabs = slabs(key_pad)
    value_slabs = slabs(value_pad)
    row_anchor = lax.axis_index("lat") * tile_rows
    query_rows = row_anchor + jnp.arange(tile_rows, dtype=jnp.int32).reshape(row_blocks, block_rows)
    window_start = jnp.clip(query_rows - RADIUS, 0, total_rows - span)
    global_key_rows = (
        row_anchor
        - RADIUS
        + block_rows * jnp.arange(row_blocks, dtype=jnp.int32)[:, None]
        + jnp.arange(key_rows, dtype=jnp.int32)[None, :]
    )
    row_inside = (global_key_rows[:, None, :] >= window_start[:, :, None]) & (
        global_key_rows[:, None, :] < window_start[:, :, None] + span
    )
    column_gap = (
        jnp.arange(slab_cols, dtype=jnp.int32)[None, :]
        - jnp.arange(block_cols, dtype=jnp.int32)[:, None]
    )
    column_inside = (column_gap >= 0) & (column_gap < span)
    allowed = row_inside[:, :, None, :, None] & column_inside[None, None, :, None, :]
    bias = jnp.where(allowed, 0.0, -1e30).astype(jnp.float32)
    bias = bias.reshape(row_blocks, block_q, block_k)
    kernel = functools.partial(
        attention_kernel,
        step=block_rows * slab_cols,
        length=block_k,
        scale=1.0 / math.sqrt(head_size),
    )
    pairs = features // lanes
    flops = 2 * 2 * 2 * block_q * block_k * lanes * row_blocks * col_blocks * pairs
    out = pl.pallas_call(
        kernel,
        out_shape=jax.ShapeDtypeStruct(query_blocks.shape, jnp.bfloat16),
        grid=(row_blocks, col_blocks, pairs),
        in_specs=[
            pl.BlockSpec((None, block_q, lanes), lambda r, c, h: (c, r, h)),
            pl.BlockSpec((None, pad_rows * slab_cols, lanes), lambda r, c, h: (c, 0, h)),
            pl.BlockSpec((None, pad_rows * slab_cols, lanes), lambda r, c, h: (c, 0, h)),
            pl.BlockSpec((None, block_q, block_k), lambda r, c, h: (r, 0, 0)),
        ],
        out_specs=pl.BlockSpec((None, block_q, lanes), lambda r, c, h: (c, r, h)),
        cost_estimate=pl.CostEstimate(
            flops=flops,
            transcendentals=2 * block_q * block_k * row_blocks * col_blocks * pairs,
            bytes_accessed=2 * (query_blocks.size * 2 + key_slabs.size * 2 * 2) + bias.size * 4,
        ),
    )(query_blocks, key_slabs, value_slabs, bias)
    out = jnp.transpose(
        out.reshape(col_blocks, row_blocks, block_rows, block_cols, features), (1, 2, 0, 3, 4)
    )
    return out.reshape(tile_rows * tile_cols, features)


def solution(mesh):
    placed = (P("lat", "lon", None), P(), P(), P(), P(), P(), P(), P(), P(), P())
    return jax.shard_map(
        shards, mesh=mesh, in_specs=placed, out_specs=P("lat", "lon", None), check_vma=False
    )
```

```python
import functools
import math

import jax
import jax.numpy as jnp
from jax import lax
from jax.sharding import PartitionSpec as P
from jax.experimental import pallas as pl

HEADS = 8
NB = 8
RADIUS = 6


HIGHEST = lax.Precision.HIGHEST
THREE_PASS = lax.Precision.HIGH


def padded_2(cells, sides, width):
    for axis, dim in sides:
        count = lax.axis_size(axis)
        head = lax.slice_in_dim(cells, 0, width, axis=dim)
        tail = lax.slice_in_dim(cells, cells.shape[dim] - width, cells.shape[dim], axis=dim)
        cells = jnp.concatenate(
            [
                lax.ppermute(tail, axis, [(i, (i + 1) % count) for i in range(count)]),
                cells,
                lax.ppermute(head, axis, [((i + 1) % count, i) for i in range(count)]),
            ],
            axis=dim,
        )
    return cells


def normed(values, gain):
    data = values.astype(jnp.float32)
    centre = jnp.mean(data, axis=-1, keepdims=True)
    centred = data - centre
    spread = jnp.mean(centred * centred, axis=-1, keepdims=True)
    return (centred * lax.rsqrt(spread + 1e-05) * gain).astype(jnp.bfloat16)


def mode_tables(total_rows, total_cols, kept_rows, kept_cols):
    factor = 1.0 / math.sqrt(total_rows * total_cols)
    column = jnp.arange(total_cols, dtype=jnp.int32)[:, None]
    lon_freq = jnp.arange(kept_cols, dtype=jnp.int32)[None, :]
    lon_angle = 2.0 * math.pi / total_cols * (column * lon_freq % total_cols).astype(jnp.float32)
    lon_cos = jnp.cos(lon_angle)
    lon_sin = jnp.sin(lon_angle)
    forward_lon = jnp.concatenate([lon_cos, -lon_sin], axis=1) * factor
    doubled = jnp.where(lon_freq == 0, 1.0, 2.0).astype(jnp.float32)
    inverse_lon = (
        jnp.concatenate(
            [jnp.transpose(lon_cos * doubled), jnp.transpose(-lon_sin * doubled)], axis=0
        )
        * factor
    )
    lat_slot = jnp.arange(kept_rows, dtype=jnp.int32)
    lat_freq = lat_slot + jnp.where(lat_slot >= kept_rows // 2, total_rows - kept_rows, 0)
    row_index = jnp.arange(total_rows, dtype=jnp.int32)[:, None]
    lat_angle = (
        2.0
        * math.pi
        / total_rows
        * (row_index * lat_freq[None, :] % total_rows).astype(jnp.float32)
    )
    return (forward_lon, inverse_lon, jnp.cos(lat_angle), jnp.sin(lat_angle))


def block_mix(inputs, weight):
    return jnp.einsum("bim,bio->bom", inputs, weight, precision=HIGHEST)


def shards(
    grid_tokens,
    attention_gain,
    score_weight,
    value_weight,
    output_weight,
    mixer_gain,
    first_weight,
    first_bias,
    second_weight,
    second_bias,
):
    tile_rows, tile_cols, features = grid_tokens.shape
    lat_count = lax.axis_size("lat")
    lon_count = lax.axis_size("lon")
    total_rows = tile_rows * lat_count
    total_cols = tile_cols * lon_count
    head_size = features // HEADS
    span = 2 * RADIUS + 1
    normed_in = normed(grid_tokens, attention_gain)
    flat_in = normed_in.reshape(tile_rows * tile_cols, features)
    queries = jnp.dot(
        flat_in, score_weight[:, :features], preferred_element_type=jnp.float32
    ).astype(jnp.bfloat16)
    queries = queries.reshape(tile_rows, tile_cols, features)
    kv_weight = jnp.concatenate([score_weight[:, features:], value_weight], axis=1)
    projected = jnp.dot(flat_in, kv_weight, preferred_element_type=jnp.float32).astype(jnp.bfloat16)
    projected = projected.reshape(tile_rows, tile_cols, 2 * features)
    padded = padded_2(projected, (("lat", 0), ("lon", 1)), RADIUS)
    key_pad = padded[:, :, :features]
    value_pad = padded[:, :, features:]
    attended = window_attention(queries, key_pad, value_pad, total_rows)
    projected_out = jnp.dot(attended, output_weight, preferred_element_type=jnp.float32)
    after_attention = (
        grid_tokens.astype(jnp.float32).reshape(-1, features) + projected_out
    ).astype(jnp.bfloat16)
    after_attention = after_attention.reshape(tile_rows, tile_cols, features)
    mixer_in = lax.optimization_barrier(normed(after_attention, mixer_gain))
    tile_back = spectral_mix(
        mixer_in, first_weight, first_bias, second_weight, second_bias
    )
    summed = (
        after_attention.astype(jnp.float32)
        + mixer_in.astype(jnp.float32)
        + tile_back.astype(jnp.float32)
    )
    return summed.astype(jnp.bfloat16)


def split_bf16(table):
    high = table.astype(jnp.bfloat16)
    return high, (table - high.astype(jnp.float32)).astype(jnp.bfloat16)


def two_pass(spec, data, table):
    high, rest = split_bf16(table)
    return jnp.einsum(spec, data, high, preferred_element_type=jnp.float32) + jnp.einsum(
        spec, data, rest, preferred_element_type=jnp.float32
    )


def spectral_mix(mixer_in, first_weight, first_bias, second_weight, second_bias):
    tile_rows, tile_cols, features = mixer_in.shape
    lat_count = lax.axis_size("lat")
    lon_count = lax.axis_size("lon")
    total_rows = tile_rows * lat_count
    total_cols = tile_cols * lon_count
    kept_rows = total_rows // 2
    kept_cols = total_cols // 4
    share = features // lon_count
    block = features // NB
    mode_share = kept_cols // lat_count
    forward_lon, inverse_lon, lat_cos, lat_sin = mode_tables(
        total_rows, total_cols, kept_rows, kept_cols
    )
    forward_lon = jnp.transpose(
        forward_lon.reshape(total_cols, 2, lat_count, mode_share), (0, 2, 1, 3)
    ).reshape(total_cols, 2 * kept_cols)
    inverse_lon = jnp.transpose(
        inverse_lon.reshape(2, lat_count, mode_share, total_cols), (1, 0, 2, 3)
    ).reshape(2 * kept_cols, total_cols)
    send = regroup(mixer_in, lon_count)
    got = lax.all_to_all(send, "lon", 0, 0, tiled=True)
    along = two_pass(
        "jf,jn->nf", got.reshape(total_cols, tile_rows * share), forward_lon
    )
    outgoing = along.astype(jnp.bfloat16).reshape(lat_count, 2 * mode_share, tile_rows * share)
    columns = lax.all_to_all(outgoing, "lat", 0, 0, tiled=True)
    columns = columns.reshape(lat_count, 2 * mode_share, tile_rows, share)
    lat_table = jnp.concatenate([lat_cos, lat_sin], axis=1).reshape(
        lat_count, tile_rows, 2 * kept_rows
    )
    both = two_pass("sqrc,srt->tqc", columns, lat_table)
    both = both.reshape(2, kept_rows, 2, mode_share, share)
    spec_real = both[0, :, 0] + both[1, :, 1]
    spec_imag = both[0, :, 1] - both[1, :, 0]
    spectrum = jnp.stack([spec_real, spec_imag])
    lon_index = lax.axis_index("lon")
    half = lon_index % 2
    block_index = lon_index // 2
    pairs = [(i, i ^ 1) for i in range(lon_count)]
    half_rows = kept_rows // 2
    own = lax.dynamic_slice_in_dim(spectrum, half * half_rows, half_rows, axis=1)
    away = lax.dynamic_slice_in_dim(spectrum, (1 - half) * half_rows, half_rows, axis=1)
    came = lax.ppermute(away, "lon", pairs)
    modes = jnp.where(
        half == 0,
        jnp.concatenate([own, came], axis=3),
        jnp.concatenate([came, own], axis=3),
    )
    w1 = lax.dynamic_index_in_dim(first_weight, block_index, axis=1, keepdims=False)
    b1 = lax.dynamic_index_in_dim(first_bias, block_index, axis=1, keepdims=False)
    w2 = lax.dynamic_index_in_dim(second_weight, block_index, axis=1, keepdims=False)
    b2 = lax.dynamic_index_in_dim(second_bias, block_index, axis=1, keepdims=False)
    real_in, imag_in = modes[0], modes[1]
    hidden_r = jax.nn.relu(mode_mix(real_in, w1[0]) - mode_mix(imag_in, w1[1]) + b1[0])
    hidden_i = jax.nn.relu(mode_mix(imag_in, w1[0]) + mode_mix(real_in, w1[1]) + b1[1])
    filtered_r = mode_mix(hidden_r, w2[0]) - mode_mix(hidden_i, w2[1]) + b2[0]
    filtered_i = mode_mix(hidden_i, w2[0]) + mode_mix(hidden_r, w2[1]) + b2[1]
    filtered = jnp.stack([filtered_r, filtered_i])
    mine = lax.dynamic_slice_in_dim(filtered, half * share, share, axis=3)
    theirs = lax.dynamic_slice_in_dim(filtered, (1 - half) * share, share, axis=3)
    back = lax.ppermute(theirs, "lon", pairs)
    returned = jnp.where(
        half == 0,
        jnp.concatenate([mine, back], axis=1),
        jnp.concatenate([back, mine], axis=1),
    )
    row_cos = lat_cos.reshape(lat_count, tile_rows, kept_rows)
    row_sin = lat_sin.reshape(lat_count, tile_rows, kept_rows)
    cos_back = jnp.einsum("ark,pkmc->apmrc", row_cos, returned, precision=THREE_PASS)
    sin_back = jnp.einsum("ark,pkmc->apmrc", row_sin, returned, precision=THREE_PASS)
    rows_real = cos_back[:, 0] - sin_back[:, 1]
    rows_imag = sin_back[:, 0] + cos_back[:, 1]
    rows = jnp.stack([rows_real, rows_imag], axis=1).astype(jnp.bfloat16)
    rows = rows.reshape(lat_count, 2 * mode_share, tile_rows * share)
    arrived = lax.all_to_all(rows, "lat", 0, 0, tiled=True)
    by_mode = arrived.reshape(2 * kept_cols, tile_rows * share)
    field = two_pass("nf,nj->jf", by_mode, inverse_lon).astype(jnp.bfloat16)
    home = lax.all_to_all(
        field.reshape(lon_count, tile_cols, tile_rows * share), "lon", 0, 0, tiled=True
    )
    return ungroup(home, tile_rows)


def regroup_kernel(x_ref, y_ref):
    rows = x_ref.shape[0]
    groups, _, width = y_ref.shape
    share = width // rows
    for g in range(groups):
        for r in range(rows):
            y_ref[g, :, r * share : (r + 1) * share] = x_ref[r, :, g * share : (g + 1) * share]


def ungroup_kernel(y_ref, x_ref):
    rows = x_ref.shape[0]
    groups, _, width = y_ref.shape
    share = width // rows
    for g in range(groups):
        for r in range(rows):
            x_ref[r, :, g * share : (g + 1) * share] = y_ref[g, :, r * share : (r + 1) * share]


def regroup(tile, groups):
    rows, cols, features = tile.shape
    return pl.pallas_call(
        regroup_kernel,
        out_shape=jax.ShapeDtypeStruct((groups, cols, rows * features // groups), tile.dtype),
        cost_estimate=pl.CostEstimate(flops=0, transcendentals=0, bytes_accessed=2 * tile.size * 2),
    )(tile)


def ungroup(grouped, rows):
    groups, cols, width = grouped.shape
    return pl.pallas_call(
        ungroup_kernel,
        out_shape=jax.ShapeDtypeStruct((rows, cols, groups * width // rows), grouped.dtype),
        cost_estimate=pl.CostEstimate(flops=0, transcendentals=0, bytes_accessed=2 * grouped.size * 2),
    )(grouped)

def mode_mix(inputs, weight):
    return jnp.einsum("kmc,co->kmo", inputs, weight, precision=HIGHEST)


def attention_kernel(q_ref, k_ref, v_ref, bias_ref, o_ref, *, step, length, scale):
    start = pl.multiple_of(pl.program_id(0) * step, 8)
    q = q_ref[...]
    k = k_ref[pl.ds(start, length), :]
    v = v_ref[pl.ds(start, length), :]
    bias = bias_ref[...]
    first = lax.broadcasted_iota(jnp.int32, q.shape, 1) < q.shape[1] // 2
    results = []
    for lanes in (first, jnp.logical_not(first)):
        head_q = jnp.where(lanes, q, jnp.zeros_like(q))
        scores = (
            lax.dot_general(
                head_q, k, (((1,), (1,)), ((), ())), preferred_element_type=jnp.float32
            )
            * scale
            + bias
        )
        largest = jnp.max(scores, axis=1, keepdims=True)
        weights = jnp.exp(scores - largest)
        probs = (weights / jnp.sum(weights, axis=1, keepdims=True)).astype(jnp.bfloat16)
        results.append(jnp.dot(probs, v, preferred_element_type=jnp.float32))
    o_ref[...] = jnp.where(first, results[0], results[1]).astype(o_ref.dtype)


def window_attention(queries, key_pad, value_pad, total_rows):
    tile_rows, tile_cols, features = queries.shape
    span = 2 * RADIUS + 1
    block_rows = 12
    block_cols = tile_cols // 2
    row_blocks = tile_rows // block_rows
    col_blocks = tile_cols // block_cols
    key_rows = block_rows + 2 * RADIUS
    key_cols = block_cols + 2 * RADIUS
    slab_cols = -(-key_cols // 8) * 8
    pad_rows = key_pad.shape[0]
    lanes = 128
    head_size = features // HEADS
    block_q = block_rows * block_cols
    block_k = key_rows * slab_cols
    query_blocks = jnp.transpose(
        queries.reshape(row_blocks, block_rows, col_blocks, block_cols, features), (2, 0, 1, 3, 4)
    ).reshape(col_blocks, row_blocks * block_q, features)

    def slabs(table):
        pieces = [
            table[:, c * block_cols : c * block_cols + key_cols] for c in range(col_blocks)
        ]
        stacked = jnp.stack(pieces)
        stacked = jnp.pad(stacked, ((0, 0), (0, 0), (0, slab_cols - key_cols), (0, 0)))
        return stacked.reshape(col_blocks, pad_rows * slab_cols, features)

    key_slabs = slabs(key_pad)
    value_slabs = slabs(value_pad)
    row_anchor = lax.axis_index("lat") * tile_rows
    shape = (row_blocks, block_q, block_k)
    block = lax.broadcasted_iota(jnp.int32, shape, 0)
    query = lax.broadcasted_iota(jnp.int32, shape, 1)
    key = lax.broadcasted_iota(jnp.int32, shape, 2)
    query_row = row_anchor + block_rows * block + query // block_cols
    window_start = jnp.clip(query_row - RADIUS, 0, total_rows - span)
    key_row = row_anchor - RADIUS + block_rows * block + key // slab_cols
    column_gap = key % slab_cols - query % block_cols
    allowed = (
        (key_row >= window_start)
        & (key_row < window_start + span)
        & (column_gap >= 0)
        & (column_gap < span)
    )
    bias = jnp.where(allowed, 0.0, -1e30).astype(jnp.float32)
    kernel = functools.partial(
        attention_kernel,
        step=block_rows * slab_cols,
        length=block_k,
        scale=1.0 / math.sqrt(head_size),
    )
    pairs = features // lanes
    flops = 2 * 2 * 2 * block_q * block_k * lanes * row_blocks * col_blocks * pairs
    out = pl.pallas_call(
        kernel,
        out_shape=jax.ShapeDtypeStruct(query_blocks.shape, jnp.bfloat16),
        grid=(row_blocks, col_blocks, pairs),
        in_specs=[
            pl.BlockSpec((None, block_q, lanes), lambda r, c, h: (c, r, h)),
            pl.BlockSpec((None, pad_rows * slab_cols, lanes), lambda r, c, h: (c, 0, h)),
            pl.BlockSpec((None, pad_rows * slab_cols, lanes), lambda r, c, h: (c, 0, h)),
            pl.BlockSpec((None, block_q, block_k), lambda r, c, h: (r, 0, 0)),
        ],
        out_specs=pl.BlockSpec((None, block_q, lanes), lambda r, c, h: (c, r, h)),
        cost_estimate=pl.CostEstimate(
            flops=flops,
            transcendentals=2 * block_q * block_k * row_blocks * col_blocks * pairs,
            bytes_accessed=2 * (query_blocks.size * 2 + key_slabs.size * 2 * 2) + bias.size * 4,
        ),
    )(query_blocks, key_slabs, value_slabs, bias)
    out = jnp.transpose(
        out.reshape(col_blocks, row_blocks, block_rows, block_cols, features), (1, 2, 0, 3, 4)
    )
    return out.reshape(tile_rows * tile_cols, features)


def solution(mesh):
    placed = (P("lat", "lon", None), P(), P(), P(), P(), P(), P(), P(), P(), P())
    return jax.shard_map(
        shards, mesh=mesh, in_specs=placed, out_specs=P("lat", "lon", None), check_vma=False
    )
```

```python
import functools
import math

import jax
import jax.numpy as jnp
from jax import lax
from jax.sharding import PartitionSpec as P
from jax.experimental import pallas as pl

HEADS = 8
NB = 8
RADIUS = 6


HIGHEST = lax.Precision.HIGHEST
THREE_PASS = lax.Precision.HIGH


def padded_2(cells, sides, width):
    (row_axis, _), (col_axis, _) = sides
    rows = lax.axis_size(row_axis)
    cols = lax.axis_size(col_axis)

    def moved(piece, down, right):
        pairs = [
            (((r - down) % rows) * cols + (c - right) % cols, r * cols + c)
            for r in range(rows)
            for c in range(cols)
        ]
        if down == 0:
            return lax.ppermute(piece, col_axis, [(i, (i + right) % cols) for i in range(cols)])
        if right == 0:
            return lax.ppermute(piece, row_axis, [(i, (i + down) % rows) for i in range(rows)])
        return lax.ppermute(piece, (row_axis, col_axis), pairs)

    top, bottom = cells[:width], cells[-width:]
    left, right = cells[:, :width], cells[:, -width:]
    upper = jnp.concatenate(
        [moved(bottom[:, -width:], 1, 1), moved(bottom, 1, 0), moved(bottom[:, :width], 1, -1)],
        axis=1,
    )
    middle = jnp.concatenate([moved(right, 0, 1), cells, moved(left, 0, -1)], axis=1)
    lower = jnp.concatenate(
        [moved(top[:, -width:], -1, 1), moved(top, -1, 0), moved(top[:, :width], -1, -1)],
        axis=1,
    )
    return jnp.concatenate([upper, middle, lower], axis=0)


def normed(values, gain):
    data = values.astype(jnp.float32)
    centre = jnp.mean(data, axis=-1, keepdims=True)
    centred = data - centre
    spread = jnp.mean(centred * centred, axis=-1, keepdims=True)
    return (centred * lax.rsqrt(spread + 1e-05) * gain).astype(jnp.bfloat16)


def mode_tables(total_rows, total_cols, kept_rows, kept_cols):
    factor = 1.0 / math.sqrt(total_rows * total_cols)
    column = jnp.arange(total_cols, dtype=jnp.int32)[:, None]
    lon_freq = jnp.arange(kept_cols, dtype=jnp.int32)[None, :]
    lon_angle = 2.0 * math.pi / total_cols * (column * lon_freq % total_cols).astype(jnp.float32)
    lon_cos = jnp.cos(lon_angle)
    lon_sin = jnp.sin(lon_angle)
    forward_lon = jnp.concatenate([lon_cos, -lon_sin], axis=1) * factor
    doubled = jnp.where(lon_freq == 0, 1.0, 2.0).astype(jnp.float32)
    inverse_lon = (
        jnp.concatenate(
            [jnp.transpose(lon_cos * doubled), jnp.transpose(-lon_sin * doubled)], axis=0
        )
        * factor
    )
    lat_slot = jnp.arange(kept_rows, dtype=jnp.int32)
    lat_freq = lat_slot + jnp.where(lat_slot >= kept_rows // 2, total_rows - kept_rows, 0)
    row_index = jnp.arange(total_rows, dtype=jnp.int32)[:, None]
    lat_angle = (
        2.0
        * math.pi
        / total_rows
        * (row_index * lat_freq[None, :] % total_rows).astype(jnp.float32)
    )
    return (forward_lon, inverse_lon, jnp.cos(lat_angle), jnp.sin(lat_angle))


def block_mix(inputs, weight):
    return jnp.einsum("bim,bio->bom", inputs, weight, precision=HIGHEST)


def shards(
    grid_tokens,
    attention_gain,
    score_weight,
    value_weight,
    output_weight,
    mixer_gain,
    first_weight,
    first_bias,
    second_weight,
    second_bias,
):
    tile_rows, tile_cols, features = grid_tokens.shape
    lat_count = lax.axis_size("lat")
    lon_count = lax.axis_size("lon")
    total_rows = tile_rows * lat_count
    total_cols = tile_cols * lon_count
    head_size = features // HEADS
    span = 2 * RADIUS + 1
    normed_in = normed(grid_tokens, attention_gain)
    flat_in = normed_in.reshape(tile_rows * tile_cols, features)
    queries = jnp.dot(
        flat_in, score_weight[:, :features], preferred_element_type=jnp.float32
    ).astype(jnp.bfloat16)
    queries = queries.reshape(tile_rows, tile_cols, features)
    kv_weight = jnp.concatenate([score_weight[:, features:], value_weight], axis=1)
    projected = jnp.dot(flat_in, kv_weight, preferred_element_type=jnp.float32).astype(jnp.bfloat16)
    projected = projected.reshape(tile_rows, tile_cols, 2 * features)
    padded = padded_2(projected, (("lat", 0), ("lon", 1)), RADIUS)
    key_pad = padded[:, :, :features]
    value_pad = padded[:, :, features:]
    attended = window_attention(queries, key_pad, value_pad, total_rows)
    projected_out = jnp.dot(attended, output_weight, preferred_element_type=jnp.float32)
    after_attention = (
        grid_tokens.astype(jnp.float32).reshape(-1, features) + projected_out
    ).astype(jnp.bfloat16)
    after_attention = after_attention.reshape(tile_rows, tile_cols, features)
    mixer_in = lax.optimization_barrier(normed(after_attention, mixer_gain))
    tile_back = spectral_mix(
        mixer_in, first_weight, first_bias, second_weight, second_bias
    )
    summed = (
        after_attention.astype(jnp.float32)
        + mixer_in.astype(jnp.float32)
        + tile_back.astype(jnp.float32)
    )
    return summed.astype(jnp.bfloat16)


def split_bf16(table):
    high = table.astype(jnp.bfloat16)
    return high, (table - high.astype(jnp.float32)).astype(jnp.bfloat16)


def two_pass(spec, data, table):
    high, rest = split_bf16(table)
    return jnp.einsum(spec, data, high, preferred_element_type=jnp.float32) + jnp.einsum(
        spec, data, rest, preferred_element_type=jnp.float32
    )


def spectral_mix(mixer_in, first_weight, first_bias, second_weight, second_bias):
    tile_rows, tile_cols, features = mixer_in.shape
    lat_count = lax.axis_size("lat")
    lon_count = lax.axis_size("lon")
    total_rows = tile_rows * lat_count
    total_cols = tile_cols * lon_count
    kept_rows = total_rows // 2
    kept_cols = total_cols // 4
    share = features // lon_count
    block = features // NB
    mode_share = kept_cols // lat_count
    forward_lon, inverse_lon, lat_cos, lat_sin = mode_tables(
        total_rows, total_cols, kept_rows, kept_cols
    )
    forward_lon = jnp.transpose(
        forward_lon.reshape(total_cols, 2, lat_count, mode_share), (0, 2, 1, 3)
    ).reshape(total_cols, 2 * kept_cols)
    inverse_lon = jnp.transpose(
        inverse_lon.reshape(2, lat_count, mode_share, total_cols), (1, 0, 2, 3)
    ).reshape(2 * kept_cols, total_cols)
    send = regroup(mixer_in, lon_count)
    got = lax.all_to_all(send, "lon", 0, 0, tiled=True)
    along = two_pass(
        "jf,jn->nf", got.reshape(total_cols, tile_rows * share), forward_lon
    )
    outgoing = along.astype(jnp.bfloat16).reshape(lat_count, 2 * mode_share, tile_rows * share)
    columns = lax.all_to_all(outgoing, "lat", 0, 0, tiled=True)
    columns = columns.reshape(lat_count, 2 * mode_share, tile_rows, share)
    lat_table = jnp.concatenate([lat_cos, lat_sin], axis=1).reshape(
        lat_count, tile_rows, 2 * kept_rows
    )
    both = two_pass("sqrc,srt->tqc", columns, lat_table)
    both = both.reshape(2, kept_rows, 2, mode_share, share)
    spec_real = both[0, :, 0] + both[1, :, 1]
    spec_imag = both[0, :, 1] - both[1, :, 0]
    spectrum = jnp.stack([spec_real, spec_imag])
    lon_index = lax.axis_index("lon")
    half = lon_index % 2
    block_index = lon_index // 2
    pairs = [(i, i ^ 1) for i in range(lon_count)]
    half_rows = kept_rows // 2
    own = lax.dynamic_slice_in_dim(spectrum, half * half_rows, half_rows, axis=1)
    away = lax.dynamic_slice_in_dim(spectrum, (1 - half) * half_rows, half_rows, axis=1)
    came = lax.ppermute(away, "lon", pairs)
    modes = jnp.where(
        half == 0,
        jnp.concatenate([own, came], axis=3),
        jnp.concatenate([came, own], axis=3),
    )
    w1 = lax.dynamic_index_in_dim(first_weight, block_index, axis=1, keepdims=False)
    b1 = lax.dynamic_index_in_dim(first_bias, block_index, axis=1, keepdims=False)
    w2 = lax.dynamic_index_in_dim(second_weight, block_index, axis=1, keepdims=False)
    b2 = lax.dynamic_index_in_dim(second_bias, block_index, axis=1, keepdims=False)
    real_in, imag_in = modes[0], modes[1]
    hidden_r = jax.nn.relu(mode_mix(real_in, w1[0]) - mode_mix(imag_in, w1[1]) + b1[0])
    hidden_i = jax.nn.relu(mode_mix(imag_in, w1[0]) + mode_mix(real_in, w1[1]) + b1[1])
    filtered_r = mode_mix(hidden_r, w2[0]) - mode_mix(hidden_i, w2[1]) + b2[0]
    filtered_i = mode_mix(hidden_i, w2[0]) + mode_mix(hidden_r, w2[1]) + b2[1]
    filtered = jnp.stack([filtered_r, filtered_i])
    mine = lax.dynamic_slice_in_dim(filtered, half * share, share, axis=3)
    theirs = lax.dynamic_slice_in_dim(filtered, (1 - half) * share, share, axis=3)
    back = lax.ppermute(theirs, "lon", pairs)
    returned = jnp.where(
        half == 0,
        jnp.concatenate([mine, back], axis=1),
        jnp.concatenate([back, mine], axis=1),
    )
    row_cos = lat_cos.reshape(lat_count, tile_rows, kept_rows)
    row_sin = lat_sin.reshape(lat_count, tile_rows, kept_rows)
    cos_back = jnp.einsum("ark,pkmc->apmrc", row_cos, returned, precision=THREE_PASS)
    sin_back = jnp.einsum("ark,pkmc->apmrc", row_sin, returned, precision=THREE_PASS)
    rows_real = cos_back[:, 0] - sin_back[:, 1]
    rows_imag = sin_back[:, 0] + cos_back[:, 1]
    rows = jnp.stack([rows_real, rows_imag], axis=1).astype(jnp.bfloat16)
    rows = rows.reshape(lat_count, 2 * mode_share, tile_rows * share)
    arrived = lax.all_to_all(rows, "lat", 0, 0, tiled=True)
    by_mode = arrived.reshape(2 * kept_cols, tile_rows * share)
    field = two_pass("nf,nj->jf", by_mode, inverse_lon).astype(jnp.bfloat16)
    home = lax.all_to_all(
        field.reshape(lon_count, tile_cols, tile_rows * share), "lon", 0, 0, tiled=True
    )
    return ungroup(home, tile_rows)


def regroup_kernel(x_ref, y_ref):
    rows = x_ref.shape[0]
    groups, _, width = y_ref.shape
    share = width // rows
    for g in range(groups):
        for r in range(rows):
            y_ref[g, :, r * share : (r + 1) * share] = x_ref[r, :, g * share : (g + 1) * share]


def ungroup_kernel(y_ref, x_ref):
    rows = x_ref.shape[0]
    groups, _, width = y_ref.shape
    share = width // rows
    for g in range(groups):
        for r in range(rows):
            x_ref[r, :, g * share : (g + 1) * share] = y_ref[g, :, r * share : (r + 1) * share]


def regroup(tile, groups):
    rows, cols, features = tile.shape
    return pl.pallas_call(
        regroup_kernel,
        out_shape=jax.ShapeDtypeStruct((groups, cols, rows * features // groups), tile.dtype),
        cost_estimate=pl.CostEstimate(flops=0, transcendentals=0, bytes_accessed=2 * tile.size * 2),
    )(tile)


def ungroup(grouped, rows):
    groups, cols, width = grouped.shape
    return pl.pallas_call(
        ungroup_kernel,
        out_shape=jax.ShapeDtypeStruct((rows, cols, groups * width // rows), grouped.dtype),
        cost_estimate=pl.CostEstimate(flops=0, transcendentals=0, bytes_accessed=2 * grouped.size * 2),
    )(grouped)

def mode_mix(inputs, weight):
    return jnp.einsum("kmc,co->kmo", inputs, weight, precision=HIGHEST)


def attention_kernel(q_ref, k_ref, v_ref, bias_ref, o_ref, *, step, length, scale):
    start = pl.multiple_of(pl.program_id(0) * step, 8)
    q = q_ref[...]
    k = k_ref[pl.ds(start, length), :]
    v = v_ref[pl.ds(start, length), :]
    bias = bias_ref[...]
    first = lax.broadcasted_iota(jnp.int32, q.shape, 1) < q.shape[1] // 2
    results = []
    for lanes in (first, jnp.logical_not(first)):
        head_q = jnp.where(lanes, q, jnp.zeros_like(q))
        scores = (
            lax.dot_general(
                head_q, k, (((1,), (1,)), ((), ())), preferred_element_type=jnp.float32
            )
            * scale
            + bias
        )
        largest = jnp.max(scores, axis=1, keepdims=True)
        weights = jnp.exp(scores - largest)
        probs = (weights / jnp.sum(weights, axis=1, keepdims=True)).astype(jnp.bfloat16)
        results.append(jnp.dot(probs, v, preferred_element_type=jnp.float32))
    o_ref[...] = jnp.where(first, results[0], results[1]).astype(o_ref.dtype)


def window_attention(queries, key_pad, value_pad, total_rows):
    tile_rows, tile_cols, features = queries.shape
    span = 2 * RADIUS + 1
    block_rows = 12
    block_cols = tile_cols // 2
    row_blocks = tile_rows // block_rows
    col_blocks = tile_cols // block_cols
    key_rows = block_rows + 2 * RADIUS
    key_cols = block_cols + 2 * RADIUS
    slab_cols = -(-key_cols // 8) * 8
    pad_rows = key_pad.shape[0]
    lanes = 128
    head_size = features // HEADS
    block_q = block_rows * block_cols
    block_k = key_rows * slab_cols
    query_blocks = jnp.transpose(
        queries.reshape(row_blocks, block_rows, col_blocks, block_cols, features), (2, 0, 1, 3, 4)
    ).reshape(col_blocks, row_blocks * block_q, features)

    def slabs(table):
        pieces = [
            table[:, c * block_cols : c * block_cols + key_cols] for c in range(col_blocks)
        ]
        stacked = jnp.stack(pieces)
        stacked = jnp.pad(stacked, ((0, 0), (0, 0), (0, slab_cols - key_cols), (0, 0)))
        return stacked.reshape(col_blocks, pad_rows * slab_cols, features)

    key_slabs = slabs(key_pad)
    value_slabs = slabs(value_pad)
    row_anchor = lax.axis_index("lat") * tile_rows
    shape = (row_blocks, block_q, block_k)
    block = lax.broadcasted_iota(jnp.int32, shape, 0)
    query = lax.broadcasted_iota(jnp.int32, shape, 1)
    key = lax.broadcasted_iota(jnp.int32, shape, 2)
    query_row = row_anchor + block_rows * block + query // block_cols
    window_start = jnp.clip(query_row - RADIUS, 0, total_rows - span)
    key_row = row_anchor - RADIUS + block_rows * block + key // slab_cols
    column_gap = key % slab_cols - query % block_cols
    allowed = (
        (key_row >= window_start)
        & (key_row < window_start + span)
        & (column_gap >= 0)
        & (column_gap < span)
    )
    bias = jnp.where(allowed, 0.0, -1e30).astype(jnp.float32)
    kernel = functools.partial(
        attention_kernel,
        step=block_rows * slab_cols,
        length=block_k,
        scale=1.0 / math.sqrt(head_size),
    )
    pairs = features // lanes
    flops = 2 * 2 * 2 * block_q * block_k * lanes * row_blocks * col_blocks * pairs
    out = pl.pallas_call(
        kernel,
        out_shape=jax.ShapeDtypeStruct(query_blocks.shape, jnp.bfloat16),
        grid=(row_blocks, col_blocks, pairs),
        in_specs=[
            pl.BlockSpec((None, block_q, lanes), lambda r, c, h: (c, r, h)),
            pl.BlockSpec((None, pad_rows * slab_cols, lanes), lambda r, c, h: (c, 0, h)),
            pl.BlockSpec((None, pad_rows * slab_cols, lanes), lambda r, c, h: (c, 0, h)),
            pl.BlockSpec((None, block_q, block_k), lambda r, c, h: (r, 0, 0)),
        ],
        out_specs=pl.BlockSpec((None, block_q, lanes), lambda r, c, h: (c, r, h)),
        cost_estimate=pl.CostEstimate(
            flops=flops,
            transcendentals=2 * block_q * block_k * row_blocks * col_blocks * pairs,
            bytes_accessed=2 * (query_blocks.size * 2 + key_slabs.size * 2 * 2) + bias.size * 4,
        ),
    )(query_blocks, key_slabs, value_slabs, bias)
    out = jnp.transpose(
        out.reshape(col_blocks, row_blocks, block_rows, block_cols, features), (1, 2, 0, 3, 4)
    )
    return out.reshape(tile_rows * tile_cols, features)


def solution(mesh):
    placed = (P("lat", "lon", None), P(), P(), P(), P(), P(), P(), P(), P(), P())
    return jax.shard_map(
        shards, mesh=mesh, in_specs=placed, out_specs=P("lat", "lon", None), check_vma=False
    )
```
